32 devices in a mesh: beam: 16 (over z, y, core), seg: 2 (over x).
Axes of the slice: x: 2, y: 2, z: 4, core: 2. Of those that a mesh axis runs over, the one named last changes fastest.
Arguments:
- surveillance: bfloat16 [16, 2, 4, 4096], P('beam', None, None, 'seg'), may hold values from -6 to 6
- reference_blocks: bfloat16 [16, 2, 4, 4096], P('beam', None, None, 'seg'), may hold values from -6 to 6
- owner_index: int32 [4], replicated, may hold values from 0 to 15
- doppler_start: int32 [16], P('beam'), may hold values from -256 to 0
- lag_blocks: int32 [16, 6], P('beam'), may hold values from -1 to 7, as said below
- block_count: int32 [16], P('beam'), may hold values from 1 to 6, as said below
Outputs:
- caf: float32 [16, 6, 2, 128, 256], P('beam', None, None, None, 'seg')
The draws below stay inside these ranges and needn't reach their ends.
Inputs may be any that keep to these rules, and one draw needn't show every extreme that they name: `block_count`: every beam lists from 1 to 6 lag blocks; some beam lists 6 and some beam lists 1. `lag_blocks`: the first block_count[b] entries of row b are distinct lag blocks; the other entries are -1.
All inputs are finite; a program needn't handle non-finite values.
Results may differ from the reference program's by a relative error of at most 0.0029.
Values may be sent and summed in bfloat16 or wider, within the bound.
No kernel may reach another device: no remote copies, remote signals or barrier semaphores. Data moves between devices by JAX's collectives and lax.ppermute only.
A program may use at most 128 MiB of HBM per device.

```python
import math
import jax
import jax.numpy as jnp
from jax import lax

LB = 128
NLB = 8
DOP = 256
DSPAN = 512
KMAX = 6
STEPS = 4
BEAMS = 16
TSTEP = 4096
TW = 16384
NLAG = 1024


def lists_and_counts(key):
    base_key = jax.random.fold_in(key, 7)
    count_key, first_key, other_key, perm_key = jax.random.split(base_key, 4)
    counts = jax.random.randint(count_key, (BEAMS,), 1, KMAX + 1)
    full_beam = jax.random.randint(first_key, (), 0, BEAMS)
    single_beam = (full_beam + 1 + jax.random.randint(other_key, (), 0, BEAMS - 1)) % BEAMS
    beam_ids = jnp.arange(BEAMS)
    counts = jnp.where(beam_ids == full_beam, KMAX, counts)
    counts = jnp.where(beam_ids == single_beam, 1, counts)
    beam_keys = jax.random.split(perm_key, BEAMS)
    shuffled = jax.vmap(lambda subkey: jax.random.permutation(subkey, NLB))(beam_keys)[:, :KMAX]
    slot_ids = jnp.arange(KMAX)[None, :]
    lists = jnp.where(slot_ids < counts[:, None], shuffled, -1)
    return (lists.astype(jnp.int32), counts.astype(jnp.int32))


def draw_lag_blocks(key, part):
    return lists_and_counts(key)[0]


def draw_block_count(key, part):
    return lists_and_counts(key)[1]


def touch_ends(entries, key, least, high):
    place = [jax.random.randint(jax.random.fold_in(key, axis), (), 0, length) for axis, length in enumerate(entries.shape)]
    longest = entries.shape.index(max(entries.shape))
    beside = place[:longest] + [(place[longest] + 1) % entries.shape[longest]] + place[longest + 1:]
    return entries.at[tuple(place)].set(least).at[tuple(beside)].set(high)


def shard_levels(own_key, dims, shards, low, top_value):
    factor_of = 1.0
    for dim, parts in shards:
        heights = jax.random.uniform(jax.random.fold_in(jax.random.fold_in(own_key, 6), dim), (parts,), jnp.float32, low / len(shards), top_value / len(shards))
        factor_of = factor_of * jnp.repeat(jnp.exp(heights), dims[dim] // parts).reshape((-1,) + (1,) * (len(dims) - 1 - dim))
    return factor_of


def scatter_about(rng, shape, width, most, cuts=(), kind=jnp.bfloat16):
    loudness = shard_levels(rng, shape, cuts, -0.22, 0.18) if cuts else 1.0
    entries = jax.random.normal(rng, shape, jnp.float32) * width * loudness
    return jnp.minimum(jnp.maximum(entries, -most), most).astype(kind)


def setup_inputs(seed: int = 0) -> dict:
    seeds = jax.random.split(jax.random.key(seed), 7)
    return {
        "surveillance": scatter_about(seeds[0], (BEAMS, 2, STEPS, TSTEP), 1.0, 6.0, ((0, 16), (3, 2))),
        "reference_blocks": scatter_about(seeds[1], (BEAMS, 2, STEPS, TSTEP), 1.0, 6.0, ((0, 16), (3, 2))),
        "owner_index": touch_ends(jax.random.randint(seeds[2], (STEPS,), 0, BEAMS), jax.random.fold_in(seeds[2], 1), 0, BEAMS - 1).astype(jnp.int32),
        "doppler_start": touch_ends(jax.random.randint(seeds[3], (BEAMS,), 0 - DSPAN // 2, DSPAN // 2 - DOP + 1), jax.random.fold_in(seeds[3], 1), 0 - DSPAN // 2, (DSPAN // 2 - DOP + 1) - 1).astype(jnp.int32),
        "lag_blocks": draw_lag_blocks(jax.random.fold_in(seeds[6], 71), 0),
        "block_count": draw_block_count(jax.random.fold_in(seeds[6], 71), 0),
    }


def modulate(samples, sample_times, freqs, window_len):
    phase_turns = jnp.mod(sample_times[:, None] * freqs[None, :], window_len)
    phase_angle = phase_turns.astype(jnp.float32) * (2.0 * math.pi / window_len)
    cos_part = jnp.cos(phase_angle)
    sine_part = jnp.sin(phase_angle)
    real_part = samples[0].astype(jnp.float32)[:, None]
    imag_part = samples[1].astype(jnp.float32)[:, None]
    c_real = (real_part * cos_part - imag_part * sine_part).astype(jnp.bfloat16)
    c_imag = (0.0 - (real_part * sine_part + imag_part * cos_part)).astype(jnp.bfloat16)
    return jnp.concatenate([c_real, c_imag], axis=1)

def hankel_rows(window, length):
    span = window.shape[1]
    lagcount = span - length
    repeated = jnp.tile(window, (1, lagcount + 1))[:, :lagcount * (span + 1)]
    shaped = repeated.reshape(2, lagcount, span + 1)[:, :, :length]
    return shaped.reshape(2 * lagcount, length)

def reference(surveillance, reference_blocks, owner_index, doppler_start, lag_blocks, block_count):
    step_len = TSTEP
    window_len = TW
    chosen = reference_blocks[owner_index, :, jnp.arange(STEPS), :]
    samples_all = jnp.transpose(chosen, (1, 0, 2)).reshape(2, window_len)
    sample_times = jnp.arange(window_len, dtype=jnp.int32)
    window_bins = jnp.arange(DOP, dtype=jnp.int32)
    normalizer = 1.0 / math.sqrt(window_len)

    def per_beam(inputs):
        signal, bin_start, blocks, listed = inputs
        coefficients = modulate(samples_all, sample_times, bin_start + window_bins, window_len)
        padded = jnp.concatenate([signal, jnp.zeros((2, STEPS, NLAG), signal.dtype)], axis=2)

        def one_slot(slot, totals):
            offset = (jnp.maximum(blocks[slot], 0) * LB).astype(jnp.int32)
            windows = lax.dynamic_slice_in_dim(padded, offset, step_len + LB, axis=2)
            hankel = jnp.concatenate([hankel_rows(windows[:, step_index], step_len) for step_index in range(STEPS)], axis=1)
            product = jnp.dot(hankel, coefficients, preferred_element_type=jnp.float32)
            real_sum = product[:LB, :DOP] - product[LB:, DOP:]
            imag_sum = product[:LB, DOP:] + product[LB:, :DOP]
            item_term = jnp.stack([real_sum, imag_sum])[None]
            return lax.dynamic_update_slice_in_dim(totals, item_term, slot, axis=0)
        totals = lax.fori_loop(0, listed, one_slot, jnp.zeros((KMAX, 2, LB, DOP), jnp.float32))
        return totals * normalizer
    return lax.map(per_beam, (surveillance, doppler_start, lag_blocks, block_count))
```

```python
import functools
import math

import jax
import jax.numpy as jnp
from jax import lax
from jax.experimental import pallas as pl
from jax.experimental.pallas import tpu as pltpu
from jax.sharding import PartitionSpec as P

LB = 128
NLB = 8
DOP = 256
CHUNK = 512


def phase_table(freqs, times, window_len):
    turns = jnp.mod(times[:, None] * freqs[None, :], window_len)
    angle = turns.astype(jnp.float32) * (2.0 * math.pi / window_len)
    return jnp.cos(angle), jnp.sin(angle)


def caf_kernel(blocks_ref, count_ref, wpad_ref, ref_ref, ac_ref, as_ref, bc_ref, bs_ref,
               out_ref, shifted, acc, *, chunks, slots, span, norm):
    k = pl.program_id(0)
    lanes = CHUNK + LB

    @pl.when(k == 0)
    def _():
        acc[...] = jnp.zeros_like(acc)

    for comp in range(2):
        def build(i, carry):
            v0 = pl.multiple_of(i * CHUNK, CHUNK)
            win = wpad_ref[k, comp:comp + 1, pl.ds(v0, lanes)]
            tile = jnp.broadcast_to(win, (LB, lanes))
            rolled = pltpu.roll(tile, lanes - LB + 1, 1, stride=1, stride_axis=0)
            shifted[comp * LB:(comp + 1) * LB, pl.ds(v0, CHUNK)] = rolled[:, :CHUNK].astype(jnp.bfloat16)
            return carry
        lax.fori_loop(0, span // CHUNK, build, 0)

    offsets = [jnp.maximum(blocks_ref[q], 0) * LB for q in range(slots)]

    def chunk(c, carry):
        g = k * chunks + c
        rr = ref_ref[g]
        r_re = rr[0:1, :]
        r_im = rr[1:2, :]
        a_c = jnp.broadcast_to(ac_ref[g], (LB, CHUNK))
        a_s = jnp.broadcast_to(as_ref[g], (LB, CHUNK))
        b_c = bc_ref[...]
        b_s = bs_ref[...]
        cos_part = a_c * b_c - a_s * b_s
        sine_part = a_s * b_c + a_c * b_s
        c_re = (r_re * cos_part - r_im * sine_part).astype(jnp.bfloat16)
        c_im = (0.0 - (r_re * sine_part + r_im * cos_part)).astype(jnp.bfloat16)
        coef = jnp.concatenate([c_re, c_im], axis=0)
        base = c * CHUNK
        for q in range(slots):
            off = pl.multiple_of(offsets[q] + base, LB)
            hank = shifted[:, pl.ds(off, CHUNK)]
            acc[q] += lax.dot_general(hank, coef, (((1,), (1,)), ((), ())),
                                      preferred_element_type=jnp.float32)
        return carry

    lax.fori_loop(0, chunks, chunk, 0)

    @pl.when(k == pl.num_programs(0) - 1)
    def _():
        count = count_ref[0]
        for q in range(slots):
            part = acc[q]
            re = part[:LB, :LB] - part[LB:, LB:]
            im = part[:LB, LB:] + part[LB:, :LB]
            keep = q < count
            out_ref[q, 0] = jnp.where(keep, re * norm, 0.0)
            out_ref[q, 1] = jnp.where(keep, im * norm, 0.0)


def shards(surveillance, reference_blocks, owner_index, doppler_start, lag_blocks, block_count):
    segments = lax.axis_size("seg")
    seg_place = lax.axis_index("seg")
    beam_place = lax.axis_index("beam")
    seg_len = surveillance.shape[3]
    step_count = surveillance.shape[2]
    step_len = seg_len * segments
    window_len = step_count * step_len
    slot_count = lag_blocks.shape[1]
    rim_len = NLB * LB
    bins = DOP // segments
    chunks = step_len // CHUNK

    mine = (owner_index == beam_place)[None, :, None]
    cleaned = lax.psum(jnp.where(mine, reference_blocks[0], jnp.zeros_like(reference_blocks[0])), "beam")
    both = jnp.stack([surveillance[0], cleaned])
    both = lax.all_gather(both, "seg", axis=3, tiled=True)
    samples = both[0]
    refs = both[1]

    span = step_len + rim_len
    wpad = jnp.transpose(samples, (1, 0, 2)).astype(jnp.float32)
    wpad = jnp.pad(wpad, ((0, 0), (0, 0), (0, span + LB - step_len)))
    refrows = jnp.transpose(refs.reshape(2, step_count * chunks, CHUNK), (1, 0, 2))
    refrows = refrows.astype(jnp.float32)

    freqs = doppler_start[0] + seg_place * bins + jnp.arange(bins, dtype=jnp.int32)
    a_c, a_s = phase_table(freqs, jnp.arange(step_count * chunks, dtype=jnp.int32) * CHUNK, window_len)
    b_c, b_s = phase_table(freqs, jnp.arange(CHUNK, dtype=jnp.int32), window_len)
    a_c = a_c[:, :, None]
    a_s = a_s[:, :, None]
    b_c = b_c.T
    b_s = b_s.T

    kernel = functools.partial(caf_kernel, chunks=chunks, slots=slot_count, span=span,
                               norm=1.0 / math.sqrt(window_len))
    full = lambda shape: pl.BlockSpec(shape, lambda k, *_: (0,) * len(shape))
    out = pl.pallas_call(
        kernel,
        out_shape=jax.ShapeDtypeStruct((slot_count, 2, LB, bins), jnp.float32),
        grid_spec=pltpu.PrefetchScalarGridSpec(
            num_scalar_prefetch=2,
            grid=(step_count,),
            in_specs=[full(wpad.shape), full(refrows.shape), full(a_c.shape), full(a_s.shape),
                      full(b_c.shape), full(b_s.shape)],
            out_specs=full((slot_count, 2, LB, bins)),
            scratch_shapes=[pltpu.VMEM((2 * LB, span), jnp.bfloat16),
                            pltpu.VMEM((slot_count, 2 * LB, 2 * bins), jnp.float32)],
        ),
        compiler_params=pltpu.CompilerParams(dimension_semantics=("arbitrary",)),
    )(lag_blocks[0], block_count, wpad, refrows, a_c, a_s, b_c, b_s)
    return jnp.flip(out, axis=2)[None]


def solution(mesh):
    placed = (
        P("beam", None, None, "seg"),
        P("beam", None, None, "seg"),
        P(),
        P("beam"),
        P("beam", None),
        P("beam"),
    )
    return jax.shard_map(
        shards,
        mesh=mesh,
        in_specs=placed,
        out_specs=P("beam", None, None, None, "seg"),
        check_vma=False,
    )
```

```python
import functools
import math

import jax
import jax.numpy as jnp
from jax import lax
from jax.experimental import pallas as pl
from jax.experimental.pallas import tpu as pltpu
from jax.sharding import PartitionSpec as P

LB = 128
NLB = 8
DOP = 256
CHUNK = 512


def phase_table(freqs, times, window_len):
    turns = jnp.mod(times[:, None] * freqs[None, :], window_len)
    angle = turns.astype(jnp.float32) * (2.0 * math.pi / window_len)
    return jnp.cos(angle), jnp.sin(angle)


def caf_kernel(blocks_ref, count_ref, wpad_ref, ref_ref, ac_ref, as_ref, bc_ref, bs_ref,
               out_ref, shifted, acc, *, chunks, slots, span, far, norm):
    k = pl.program_id(0)
    lanes = CHUNK + LB

    @pl.when(k == 0)
    def _():
        acc[...] = jnp.zeros_like(acc)

    for comp in range(2):
        def build(i, carry):
            v0 = pl.multiple_of(i * CHUNK, CHUNK)
            win = wpad_ref[k, comp:comp + 1, pl.ds(v0, lanes)]
            tile = jnp.broadcast_to(win, (LB, lanes))
            rolled = pltpu.roll(tile, lanes - LB + 1, 1, stride=1, stride_axis=0)
            shifted[comp * LB:(comp + 1) * LB, pl.ds(v0, CHUNK)] = rolled[:, :CHUNK].astype(jnp.bfloat16)
            return carry
        lax.fori_loop(0, span // CHUNK, build, 0)

    offsets = [jnp.maximum(blocks_ref[q], 0) * LB for q in range(slots)]

    def chunk(c, carry):
        g = k * chunks + c
        rr = ref_ref[g]
        r_re = rr[0:1, :]
        r_im = rr[1:2, :]
        a_c = jnp.broadcast_to(ac_ref[g], (LB, CHUNK))
        a_s = jnp.broadcast_to(as_ref[g], (LB, CHUNK))
        b_c = bc_ref[...]
        b_s = bs_ref[...]
        cos_part = a_c * b_c - a_s * b_s
        sine_part = a_s * b_c + a_c * b_s
        c_re = (r_re * cos_part - r_im * sine_part).astype(jnp.bfloat16)
        c_im = (0.0 - (r_re * sine_part + r_im * cos_part)).astype(jnp.bfloat16)
        coef = jnp.concatenate([c_re, c_im], axis=0)
        base = far - c * CHUNK
        for q in range(slots):
            off = pl.multiple_of(base - offsets[q], LB)
            hank = shifted[:, pl.ds(off, CHUNK)]
            acc[q] += lax.dot_general(hank, coef, (((1,), (1,)), ((), ())),
                                      preferred_element_type=jnp.float32)
        return carry

    lax.fori_loop(0, chunks, chunk, 0)

    @pl.when(k == pl.num_programs(0) - 1)
    def _():
        count = count_ref[0]
        for q in range(slots):
            part = acc[q]
            re = part[:LB, :LB] - part[LB:, LB:]
            im = part[:LB, LB:] + part[LB:, :LB]
            keep = q < count
            out_ref[q, 0] = jnp.where(keep, re * norm, 0.0)
            out_ref[q, 1] = jnp.where(keep, im * norm, 0.0)


def butterfly_sum(value, axis):
    count = lax.axis_size(axis)
    if count & (count - 1):
        return lax.psum(value, axis)
    bit = 1
    while bit < count:
        value = value + lax.ppermute(value, axis, [(i, i ^ bit) for i in range(count)])
        bit *= 2
    return value


def seg_join(half, axis):
    count = lax.axis_size(axis)
    parts = lax.all_gather(half, axis, axis=half.ndim - 1, tiled=True) if count != 2 else None
    if parts is not None:
        return parts
    other = lax.ppermute(half, axis, [(0, 1), (1, 0)])
    first = lax.axis_index(axis) == 0
    return jnp.where(first, jnp.concatenate([half, other], -1), jnp.concatenate([other, half], -1))


def shards(surveillance, reference_blocks, owner_index, doppler_start, lag_blocks, block_count):
    segments = lax.axis_size("seg")
    seg_place = lax.axis_index("seg")
    beam_place = lax.axis_index("beam")
    seg_len = surveillance.shape[3]
    step_count = surveillance.shape[2]
    step_len = seg_len * segments
    window_len = step_count * step_len
    slot_count = lag_blocks.shape[1]
    rim_len = NLB * LB
    bins = DOP // segments
    chunks = step_len // CHUNK

    samples = seg_join(surveillance[0], "seg")
    mine = (owner_index == beam_place)[None, :, None]
    cleaned = butterfly_sum(jnp.where(mine, reference_blocks[0], jnp.zeros_like(reference_blocks[0])), "beam")
    refs = seg_join(cleaned, "seg")

    span = step_len + rim_len
    far = rim_len - LB + step_len - CHUNK
    lead = far + CHUNK + LB - 2 - (step_len - 1)
    wpad = jnp.flip(jnp.transpose(samples, (1, 0, 2)), axis=2).astype(jnp.float32)
    wpad = jnp.pad(wpad, ((0, 0), (0, 0), (lead, span + LB - step_len - lead)))
    refrows = jnp.flip(jnp.transpose(refs.reshape(2, step_count * chunks, CHUNK), (1, 0, 2)), axis=2)
    refrows = refrows.astype(jnp.float32)

    freqs = doppler_start[0] + seg_place * bins + jnp.arange(bins, dtype=jnp.int32)
    a_c, a_s = phase_table(freqs, jnp.arange(step_count * chunks, dtype=jnp.int32) * CHUNK, window_len)
    fine = 64
    h_c, h_s = phase_table(freqs, jnp.arange(CHUNK // fine, dtype=jnp.int32) * fine, window_len)
    l_c, l_s = phase_table(freqs, jnp.arange(fine, dtype=jnp.int32), window_len)
    b_c = (h_c[:, None] * l_c[None] - h_s[:, None] * l_s[None]).reshape(CHUNK, bins)
    b_s = (h_s[:, None] * l_c[None] + h_c[:, None] * l_s[None]).reshape(CHUNK, bins)
    a_c = a_c[:, :, None]
    a_s = a_s[:, :, None]
    b_c = jnp.flip(b_c, axis=0).T
    b_s = jnp.flip(b_s, axis=0).T

    kernel = functools.partial(caf_kernel, chunks=chunks, slots=slot_count, span=span, far=far,
                               norm=1.0 / math.sqrt(window_len))
    full = lambda shape: pl.BlockSpec(shape, lambda k, *_: (0,) * len(shape))
    out = pl.pallas_call(
        kernel,
        out_shape=jax.ShapeDtypeStruct((slot_count, 2, LB, bins), jnp.float32),
        grid_spec=pltpu.PrefetchScalarGridSpec(
            num_scalar_prefetch=2,
            grid=(step_count,),
            in_specs=[full(wpad.shape), full(refrows.shape), full(a_c.shape), full(a_s.shape),
                      full(b_c.shape), full(b_s.shape)],
            out_specs=full((slot_count, 2, LB, bins)),
            scratch_shapes=[pltpu.VMEM((2 * LB, span), jnp.bfloat16),
                            pltpu.VMEM((slot_count, 2 * LB, 2 * bins), jnp.float32)],
        ),
        compiler_params=pltpu.CompilerParams(dimension_semantics=("arbitrary",)),
    )(lag_blocks[0], block_count, wpad, refrows, a_c, a_s, b_c, b_s)
    return out[None]


def solution(mesh):
    placed = (
        P("beam", None, None, "seg"),
        P("beam", None, None, "seg"),
        P(),
        P("beam"),
        P("beam", None),
        P("beam"),
    )
    return jax.shard_map(
        shards,
        mesh=mesh,
        in_specs=placed,
        out_specs=P("beam", None, None, None, "seg"),
        check_vma=False,
    )
```

```python
import functools
import math

import jax
import jax.numpy as jnp
from jax import lax
from jax.experimental import pallas as pl
from jax.experimental.pallas import tpu as pltpu
from jax.sharding import PartitionSpec as P

LB = 128
NLB = 8
DOP = 256
CHUNK = 512


def phase_table(freqs, times, window_len):
    turns = jnp.mod(times[:, None] * freqs[None, :], window_len)
    angle = turns.astype(jnp.float32) * (2.0 * math.pi / window_len)
    return jnp.cos(angle), jnp.sin(angle)


def reverse_rows(x):
    n = x.shape[0]
    rows = lax.broadcasted_iota(jnp.int32, (n, n), 0)
    cols = lax.broadcasted_iota(jnp.int32, (n, n), 1)
    flip = jnp.where(rows + cols == n - 1, 1.0, 0.0).astype(jnp.bfloat16)
    high = x.astype(jnp.bfloat16)
    rest = x - high.astype(jnp.float32)
    mid = rest.astype(jnp.bfloat16)
    low = (rest - mid.astype(jnp.float32)).astype(jnp.bfloat16)
    turn = lambda piece: jnp.dot(flip, piece, preferred_element_type=jnp.float32)
    return (turn(high) + turn(mid)) + turn(low)


def caf_kernel(blocks_ref, count_ref, wpad_ref, ref_ref, ac_ref, as_ref, bc_ref, bs_ref,
               out_ref, shifted, acc, *, chunks, slots, span, norm):
    k = pl.program_id(0)
    lanes = CHUNK + LB

    @pl.when(k == 0)
    def _():
        acc[...] = jnp.zeros_like(acc)

    for comp in range(2):
        def build(i, carry):
            v0 = pl.multiple_of(i * CHUNK, CHUNK)
            win = wpad_ref[k, comp:comp + 1, pl.ds(v0, lanes)]
            tile = jnp.broadcast_to(win, (LB, lanes))
            rolled = pltpu.roll(tile, lanes - LB + 1, 1, stride=1, stride_axis=0)
            shifted[comp * LB:(comp + 1) * LB, pl.ds(v0, CHUNK)] = rolled[:, :CHUNK].astype(jnp.bfloat16)
            return carry
        lax.fori_loop(0, span // CHUNK, build, 0)

    offsets = [jnp.maximum(blocks_ref[q], 0) * LB for q in range(slots)]

    def chunk(c, carry):
        g = k * chunks + c
        rr = ref_ref[g]
        r_re = rr[0:1, :]
        r_im = rr[1:2, :]
        a_c = jnp.broadcast_to(ac_ref[g], (LB, CHUNK))
        a_s = jnp.broadcast_to(as_ref[g], (LB, CHUNK))
        b_c = bc_ref[...]
        b_s = bs_ref[...]
        cos_part = a_c * b_c - a_s * b_s
        sine_part = a_s * b_c + a_c * b_s
        c_re = (r_re * cos_part - r_im * sine_part).astype(jnp.bfloat16)
        c_im = (0.0 - (r_re * sine_part + r_im * cos_part)).astype(jnp.bfloat16)
        coef = jnp.concatenate([c_re, c_im], axis=0)
        base = c * CHUNK
        for q in range(slots):
            off = pl.multiple_of(offsets[q] + base, LB)
            hank = shifted[:, pl.ds(off, CHUNK)]
            acc[q] += lax.dot_general(hank, coef, (((1,), (1,)), ((), ())),
                                      preferred_element_type=jnp.float32)
        return carry

    lax.fori_loop(0, chunks, chunk, 0)

    @pl.when(k == pl.num_programs(0) - 1)
    def _():
        count = count_ref[0]
        for q in range(slots):
            part = acc[q]
            re = part[:LB, :LB] - part[LB:, LB:]
            im = part[:LB, LB:] + part[LB:, :LB]
            keep = q < count
            out_ref[q, 0] = jnp.where(keep, reverse_rows(re) * norm, 0.0)
            out_ref[q, 1] = jnp.where(keep, reverse_rows(im) * norm, 0.0)


def butterfly_sum(value, axes):
    count = lax.axis_size(axes)
    if count & (count - 1):
        return lax.psum(value, axes)
    stride = 1
    while stride < count:
        radix = 4 if stride * 4 <= count else 2
        parts = [lax.ppermute(value, axes, [(i, i ^ (m * stride)) for i in range(count)]) for m in range(1, radix)]
        for part in parts:
            value = value + part
        stride *= radix
    return value


def seg_join(half, axis):
    count = lax.axis_size(axis)
    parts = lax.all_gather(half, axis, axis=half.ndim - 1, tiled=True) if count != 2 else None
    if parts is not None:
        return parts
    other = lax.ppermute(half, axis, [(0, 1), (1, 0)])
    first = lax.axis_index(axis) == 0
    return jnp.where(first, jnp.concatenate([half, other], -1), jnp.concatenate([other, half], -1))


def shards(surveillance, reference_blocks, owner_index, doppler_start, lag_blocks, block_count):
    segments = lax.axis_size("seg")
    seg_place = lax.axis_index("seg")
    beam_place = lax.axis_index("beam")
    seg_len = surveillance.shape[3]
    step_count = surveillance.shape[2]
    step_len = seg_len * segments
    window_len = step_count * step_len
    slot_count = lag_blocks.shape[1]
    rim_len = NLB * LB
    bins = DOP // segments
    chunks = step_len // CHUNK

    samples = seg_join(surveillance[0], "seg")
    mine = (owner_index == beam_place)[None, :, None]
    local = jnp.where(mine, reference_blocks[0], jnp.zeros_like(reference_blocks[0]))
    if segments == 2:
        first = seg_place == 0
        zero = jnp.zeros_like(local)
        placed = jnp.where(first, jnp.concatenate([local, zero], -1), jnp.concatenate([zero, local], -1))
        refs = butterfly_sum(placed, ("beam", "seg"))
    else:
        refs = seg_join(butterfly_sum(local, "beam"), "seg")

    span = step_len + rim_len
    wpad = jnp.transpose(samples, (1, 0, 2)).astype(jnp.float32)
    wpad = jnp.pad(wpad, ((0, 0), (0, 0), (0, span + LB - step_len)))
    refrows = jnp.transpose(refs.reshape(2, step_count * chunks, CHUNK), (1, 0, 2)).astype(jnp.float32)

    freqs = doppler_start[0] + seg_place * bins + jnp.arange(bins, dtype=jnp.int32)
    fine = 64
    a_c, a_s = phase_table(freqs, jnp.arange(step_count * chunks, dtype=jnp.int32) * CHUNK, window_len)
    h_c, h_s = phase_table(freqs, jnp.arange(CHUNK // fine, dtype=jnp.int32) * fine, window_len)
    l_c, l_s = phase_table(freqs, jnp.arange(fine, dtype=jnp.int32), window_len)
    a_c, a_s, h_c, h_s, l_c, l_s = lax.optimization_barrier((a_c, a_s, h_c, h_s, l_c, l_s))
    b_c = (h_c[:, None] * l_c[None] - h_s[:, None] * l_s[None]).reshape(CHUNK, bins).T
    b_s = (h_s[:, None] * l_c[None] + h_c[:, None] * l_s[None]).reshape(CHUNK, bins).T
    a_c = a_c[:, :, None]
    a_s = a_s[:, :, None]

    kernel = functools.partial(caf_kernel, chunks=chunks, slots=slot_count, span=span,
                               norm=1.0 / math.sqrt(window_len))
    full = lambda shape: pl.BlockSpec(shape, lambda k, *_: (0,) * len(shape))
    out = pl.pallas_call(
        kernel,
        out_shape=jax.ShapeDtypeStruct((slot_count, 2, LB, bins), jnp.float32),
        grid_spec=pltpu.PrefetchScalarGridSpec(
            num_scalar_prefetch=2,
            grid=(step_count,),
            in_specs=[full(wpad.shape), full(refrows.shape), full(a_c.shape), full(a_s.shape),
                      full(b_c.shape), full(b_s.shape)],
            out_specs=full((slot_count, 2, LB, bins)),
            scratch_shapes=[pltpu.VMEM((2 * LB, span), jnp.bfloat16),
                            pltpu.VMEM((slot_count, 2 * LB, 2 * bins), jnp.float32)],
        ),
        compiler_params=pltpu.CompilerParams(dimension_semantics=("arbitrary",)),
    )(lag_blocks[0], block_count, wpad, refrows, a_c, a_s, b_c, b_s)
    return out[None]


def solution(mesh):
    placed = (
        P("beam", None, None, "seg"),
        P("beam", None, None, "seg"),
        P(),
        P("beam"),
        P("beam", None),
        P("beam"),
    )
    return jax.shard_map(
        shards,
        mesh=mesh,
        in_specs=placed,
        out_specs=P("beam", None, None, None, "seg"),
        check_vma=False,
    )
```

```python
import functools
import math

import jax
import jax.numpy as jnp
from jax import lax
from jax.experimental import pallas as pl
from jax.experimental.pallas import tpu as pltpu
from jax.sharding import PartitionSpec as P

LB = 128
NLB = 8
DOP = 256
CHUNK = 2048
PIECE = 1024


def phase_table(freqs, times, window_len):
    turns = jnp.mod(times[:, None] * freqs[None, :], window_len)
    angle = turns.astype(jnp.float32) * (2.0 * math.pi / window_len)
    return jnp.cos(angle), jnp.sin(angle)


def reverse_rows(x):
    n = x.shape[0]
    rows = lax.broadcasted_iota(jnp.int32, (n, n), 0)
    cols = lax.broadcasted_iota(jnp.int32, (n, n), 1)
    flip = jnp.where(rows + cols == n - 1, 1.0, 0.0).astype(jnp.bfloat16)
    high = x.astype(jnp.bfloat16)
    rest = x - high.astype(jnp.float32)
    mid = rest.astype(jnp.bfloat16)
    low = (rest - mid.astype(jnp.float32)).astype(jnp.bfloat16)
    turn = lambda piece: jnp.dot(flip, piece, preferred_element_type=jnp.float32)
    return (turn(high) + turn(mid)) + turn(low)


def caf_kernel(blocks_ref, count_ref, wpad_ref, ref_ref, ac_ref, as_ref, bc_ref, bs_ref,
               out_ref, shifted, acc, *, chunks, slots, span, norm):
    k = pl.program_id(0)
    lanes = PIECE + LB

    @pl.when(k == 0)
    def _():
        acc[...] = jnp.zeros_like(acc)

    for comp in range(2):
        def build(i, carry):
            v0 = pl.multiple_of(i * PIECE, PIECE)
            win = wpad_ref[k, comp:comp + 1, pl.ds(v0, lanes)]
            tile = jnp.broadcast_to(win, (LB, lanes))
            rolled = pltpu.roll(tile, lanes - LB + 1, 1, stride=1, stride_axis=0)
            shifted[comp * LB:(comp + 1) * LB, pl.ds(v0, PIECE)] = rolled[:, :PIECE].astype(jnp.bfloat16)
            return carry
        lax.fori_loop(0, span // PIECE, build, 0)

    offsets = [jnp.maximum(blocks_ref[q], 0) * LB for q in range(slots)]

    def chunk(c, carry):
        g = k * chunks + c
        rr = ref_ref[g]
        r_re = rr[0:1, :]
        r_im = rr[1:2, :]
        a_c = jnp.broadcast_to(ac_ref[g], (LB, CHUNK))
        a_s = jnp.broadcast_to(as_ref[g], (LB, CHUNK))
        b_c = bc_ref[...]
        b_s = bs_ref[...]
        cos_part = a_c * b_c - a_s * b_s
        sine_part = a_s * b_c + a_c * b_s
        c_re = (r_re * cos_part - r_im * sine_part).astype(jnp.bfloat16)
        c_im = (0.0 - (r_re * sine_part + r_im * cos_part)).astype(jnp.bfloat16)
        coef = jnp.concatenate([c_re, c_im], axis=0)
        base = c * CHUNK
        for q in range(slots):
            off = pl.multiple_of(offsets[q] + base, LB)
            hank = shifted[:, pl.ds(off, CHUNK)]
            acc[q] += lax.dot_general(hank, coef, (((1,), (1,)), ((), ())),
                                      preferred_element_type=jnp.float32)
        return carry

    lax.fori_loop(0, chunks, chunk, 0)

    @pl.when(k == pl.num_programs(0) - 1)
    def _():
        count = count_ref[0]
        for q in range(slots):
            part = acc[q]
            re = part[:LB, :LB] - part[LB:, LB:]
            im = part[:LB, LB:] + part[LB:, :LB]
            keep = q < count
            out_ref[q, 0] = jnp.where(keep, reverse_rows(re) * norm, 0.0)
            out_ref[q, 1] = jnp.where(keep, reverse_rows(im) * norm, 0.0)


def butterfly_sum(value, axes):
    count = lax.axis_size(axes)
    if count & (count - 1):
        return lax.psum(value, axes)
    stride = 1
    while stride < count:
        radix = 4 if stride * 4 <= count else 2
        parts = [lax.ppermute(value, axes, [(i, i ^ (m * stride)) for i in range(count)]) for m in range(1, radix)]
        for part in parts:
            value = value + part
        stride *= radix
    return value


def seg_join(half, axis):
    count = lax.axis_size(axis)
    parts = lax.all_gather(half, axis, axis=half.ndim - 1, tiled=True) if count != 2 else None
    if parts is not None:
        return parts
    other = lax.ppermute(half, axis, [(0, 1), (1, 0)])
    first = lax.axis_index(axis) == 0
    return jnp.where(first, jnp.concatenate([half, other], -1), jnp.concatenate([other, half], -1))


def shards(surveillance, reference_blocks, owner_index, doppler_start, lag_blocks, block_count):
    segments = lax.axis_size("seg")
    seg_place = lax.axis_index("seg")
    beam_place = lax.axis_index("beam")
    seg_len = surveillance.shape[3]
    step_count = surveillance.shape[2]
    step_len = seg_len * segments
    window_len = step_count * step_len
    slot_count = lag_blocks.shape[1]
    rim_len = NLB * LB
    bins = DOP // segments
    chunks = step_len // CHUNK

    samples = seg_join(surveillance[0], "seg")
    mine = (owner_index == beam_place)[None, :, None]
    local = jnp.where(mine, reference_blocks[0], jnp.zeros_like(reference_blocks[0]))
    if segments == 2:
        first = seg_place == 0
        zero = jnp.zeros_like(local)
        placed = jnp.where(first, jnp.concatenate([local, zero], -1), jnp.concatenate([zero, local], -1))
        refs = butterfly_sum(placed, ("beam", "seg"))
    else:
        refs = seg_join(butterfly_sum(local, "beam"), "seg")

    span = step_len + rim_len
    wpad = jnp.transpose(samples, (1, 0, 2)).astype(jnp.float32)
    wpad = jnp.pad(wpad, ((0, 0), (0, 0), (0, span + LB - step_len)))
    refrows = jnp.transpose(refs.reshape(2, step_count * chunks, CHUNK), (1, 0, 2)).astype(jnp.float32)

    freqs = doppler_start[0] + seg_place * bins + jnp.arange(bins, dtype=jnp.int32)
    fine = 64
    a_c, a_s = phase_table(freqs, jnp.arange(step_count * chunks, dtype=jnp.int32) * CHUNK, window_len)
    h_c, h_s = phase_table(freqs, jnp.arange(CHUNK // fine, dtype=jnp.int32) * fine, window_len)
    l_c, l_s = phase_table(freqs, jnp.arange(fine, dtype=jnp.int32), window_len)
    a_c, a_s, h_c, h_s, l_c, l_s = lax.optimization_barrier((a_c, a_s, h_c, h_s, l_c, l_s))
    b_c = (h_c[:, None] * l_c[None] - h_s[:, None] * l_s[None]).reshape(CHUNK, bins).T
    b_s = (h_s[:, None] * l_c[None] + h_c[:, None] * l_s[None]).reshape(CHUNK, bins).T
    a_c = a_c[:, :, None]
    a_s = a_s[:, :, None]

    kernel = functools.partial(caf_kernel, chunks=chunks, slots=slot_count, span=span,
                               norm=1.0 / math.sqrt(window_len))
    full = lambda shape: pl.BlockSpec(shape, lambda k, *_: (0,) * len(shape))
    out = pl.pallas_call(
        kernel,
        out_shape=jax.ShapeDtypeStruct((slot_count, 2, LB, bins), jnp.float32),
        grid_spec=pltpu.PrefetchScalarGridSpec(
            num_scalar_prefetch=2,
            grid=(step_count,),
            in_specs=[full(wpad.shape), full(refrows.shape), full(a_c.shape), full(a_s.shape),
                      full(b_c.shape), full(b_s.shape)],
            out_specs=full((slot_count, 2, LB, bins)),
            scratch_shapes=[pltpu.VMEM((2 * LB, span), jnp.bfloat16),
                            pltpu.VMEM((slot_count, 2 * LB, 2 * bins), jnp.float32)],
        ),
        compiler_params=pltpu.CompilerParams(dimension_semantics=("arbitrary",)),
    )(lag_blocks[0], block_count, wpad, refrows, a_c, a_s, b_c, b_s)
    return out[None]


def solution(mesh):
    placed = (
        P("beam", None, None, "seg"),
        P("beam", None, None, "seg"),
        P(),
        P("beam"),
        P("beam", None),
        P("beam"),
    )
    return jax.shard_map(
        shards,
        mesh=mesh,
        in_specs=placed,
        out_specs=P("beam", None, None, None, "seg"),
        check_vma=False,
    )
```

```python
import functools
import math

import jax
import jax.numpy as jnp
from jax import lax
from jax.experimental import pallas as pl
from jax.experimental.pallas import tpu as pltpu
from jax.sharding import PartitionSpec as P

LB = 128
NLB = 8
DOP = 256
CHUNK = 2048
PIECE = 1024


def phase_table(freqs, times, window_len):
    turns = jnp.mod(times[:, None] * freqs[None, :], window_len)
    angle = turns.astype(jnp.float32) * (2.0 * math.pi / window_len)
    return jnp.cos(angle), jnp.sin(angle)


def reverse_rows(x):
    n = x.shape[0]
    rows = lax.broadcasted_iota(jnp.int32, (n, n), 0)
    cols = lax.broadcasted_iota(jnp.int32, (n, n), 1)
    flip = jnp.where(rows + cols == n - 1, 1.0, 0.0).astype(jnp.bfloat16)
    high = x.astype(jnp.bfloat16)
    rest = x - high.astype(jnp.float32)
    mid = rest.astype(jnp.bfloat16)
    low = (rest - mid.astype(jnp.float32)).astype(jnp.bfloat16)
    turn = lambda piece: jnp.dot(flip, piece, preferred_element_type=jnp.float32)
    return (turn(high) + turn(mid)) + turn(low)


def caf_kernel(blocks_ref, count_ref, wpad_ref, ref_ref, ac_ref, as_ref, bc_ref, bs_ref,
               out_ref, first_buf, second_buf, acc, *, chunks, slots, span, steps, norm):
    pair = pl.program_id(0)
    lanes = PIECE + LB
    pieces = [(comp, i) for comp in range(2) for i in range(span // PIECE)]
    share = -(-len(pieces) // chunks)

    def build_piece(step, comp, i, dst):
        v0 = i * PIECE
        win = wpad_ref[step, comp:comp + 1, v0:v0 + lanes]
        tile = jnp.broadcast_to(win, (LB, lanes))
        rolled = pltpu.roll(tile, lanes - LB + 1, 1, stride=1, stride_axis=0)
        dst[comp * LB:(comp + 1) * LB, v0:v0 + PIECE] = rolled[:, :PIECE].astype(jnp.bfloat16)

    @pl.when(pair == 0)
    def _():
        acc[...] = jnp.zeros_like(acc)
        for comp, i in pieces:
            build_piece(0, comp, i, first_buf)

    offsets = [jnp.maximum(blocks_ref[q], 0) * LB for q in range(slots)]

    def one_step(step, cur, nxt, next_step):
        for c in range(chunks):
            g = step * chunks + c
            rr = ref_ref[g]
            r_re = rr[0:1, :]
            r_im = rr[1:2, :]
            a_c = jnp.broadcast_to(ac_ref[g], (LB, CHUNK))
            a_s = jnp.broadcast_to(as_ref[g], (LB, CHUNK))
            b_c = bc_ref[...]
            b_s = bs_ref[...]
            cos_part = a_c * b_c - a_s * b_s
            sine_part = a_s * b_c + a_c * b_s
            c_re = (r_re * cos_part - r_im * sine_part).astype(jnp.bfloat16)
            c_im = (0.0 - (r_re * sine_part + r_im * cos_part)).astype(jnp.bfloat16)
            coef = jnp.concatenate([c_re, c_im], axis=0)
            for q in range(slots):
                off = pl.multiple_of(offsets[q] + c * CHUNK, LB)
                hank = cur[:, pl.ds(off, CHUNK)]
                acc[q] += lax.dot_general(hank, coef, (((1,), (1,)), ((), ())),
                                          preferred_element_type=jnp.float32)
            for comp, i in pieces[c * share:(c + 1) * share]:
                build_piece(next_step, comp, i, nxt)

    step = 2 * pair
    one_step(step, first_buf, second_buf, step + 1)
    one_step(step + 1, second_buf, first_buf, jnp.minimum(step + 2, steps - 1))

    @pl.when(pair == pl.num_programs(0) - 1)
    def _():
        count = count_ref[0]
        for q in range(slots):
            part = acc[q]
            re = part[:LB, :LB] - part[LB:, LB:]
            im = part[:LB, LB:] + part[LB:, :LB]
            keep = q < count
            out_ref[q, 0] = jnp.where(keep, reverse_rows(re) * norm, 0.0)
            out_ref[q, 1] = jnp.where(keep, reverse_rows(im) * norm, 0.0)


def butterfly_sum(value, axes):
    count = lax.axis_size(axes)
    if count & (count - 1):
        return lax.psum(value, axes)
    stride = 1
    while stride < count:
        radix = 4 if stride * 4 <= count else 2
        parts = [lax.ppermute(value, axes, [(i, i ^ (m * stride)) for i in range(count)]) for m in range(1, radix)]
        for part in parts:
            value = value + part
        stride *= radix
    return value


def seg_join(half, axis):
    count = lax.axis_size(axis)
    parts = lax.all_gather(half, axis, axis=half.ndim - 1, tiled=True) if count != 2 else None
    if parts is not None:
        return parts
    other = lax.ppermute(half, axis, [(0, 1), (1, 0)])
    first = lax.axis_index(axis) == 0
    return jnp.where(first, jnp.concatenate([half, other], -1), jnp.concatenate([other, half], -1))


def shards(surveillance, reference_blocks, owner_index, doppler_start, lag_blocks, block_count):
    segments = lax.axis_size("seg")
    seg_place = lax.axis_index("seg")
    beam_place = lax.axis_index("beam")
    seg_len = surveillance.shape[3]
    step_count = surveillance.shape[2]
    step_len = seg_len * segments
    window_len = step_count * step_len
    slot_count = lag_blocks.shape[1]
    rim_len = NLB * LB
    bins = DOP // segments
    chunks = step_len // CHUNK

    samples = seg_join(surveillance[0], "seg")
    mine = (owner_index == beam_place)[None, :, None]
    local = jnp.where(mine, reference_blocks[0], jnp.zeros_like(reference_blocks[0]))
    if segments == 2:
        first = seg_place == 0
        zero = jnp.zeros_like(local)
        placed = jnp.where(first, jnp.concatenate([local, zero], -1), jnp.concatenate([zero, local], -1))
        refs = butterfly_sum(placed, ("beam", "seg"))
    else:
        refs = seg_join(butterfly_sum(local, "beam"), "seg")

    span = step_len + rim_len
    wpad = jnp.transpose(samples, (1, 0, 2)).astype(jnp.float32)
    wpad = jnp.pad(wpad, ((0, 0), (0, 0), (0, span + LB - step_len)))
    refrows = jnp.transpose(refs.reshape(2, step_count * chunks, CHUNK), (1, 0, 2)).astype(jnp.float32)

    freqs = doppler_start[0] + seg_place * bins + jnp.arange(bins, dtype=jnp.int32)
    fine = 64
    a_c, a_s = phase_table(freqs, jnp.arange(step_count * chunks, dtype=jnp.int32) * CHUNK, window_len)
    h_c, h_s = phase_table(freqs, jnp.arange(CHUNK // fine, dtype=jnp.int32) * fine, window_len)
    l_c, l_s = phase_table(freqs, jnp.arange(fine, dtype=jnp.int32), window_len)
    a_c, a_s, h_c, h_s, l_c, l_s = lax.optimization_barrier((a_c, a_s, h_c, h_s, l_c, l_s))
    b_c = (h_c[:, None] * l_c[None] - h_s[:, None] * l_s[None]).reshape(CHUNK, bins).T
    b_s = (h_s[:, None] * l_c[None] + h_c[:, None] * l_s[None]).reshape(CHUNK, bins).T
    a_c = a_c[:, :, None]
    a_s = a_s[:, :, None]

    assert step_count % 2 == 0
    kernel = functools.partial(caf_kernel, chunks=chunks, slots=slot_count, span=span, steps=step_count,
                               norm=1.0 / math.sqrt(window_len))
    full = lambda shape: pl.BlockSpec(shape, lambda k, *_: (0,) * len(shape))
    out = pl.pallas_call(
        kernel,
        out_shape=jax.ShapeDtypeStruct((slot_count, 2, LB, bins), jnp.float32),
        grid_spec=pltpu.PrefetchScalarGridSpec(
            num_scalar_prefetch=2,
            grid=(step_count // 2,),
            in_specs=[full(wpad.shape), full(refrows.shape), full(a_c.shape), full(a_s.shape),
                      full(b_c.shape), full(b_s.shape)],
            out_specs=full((slot_count, 2, LB, bins)),
            scratch_shapes=[pltpu.VMEM((2 * LB, span), jnp.bfloat16), pltpu.VMEM((2 * LB, span), jnp.bfloat16),
                            pltpu.VMEM((slot_count, 2 * LB, 2 * bins), jnp.float32)],
        ),
        compiler_params=pltpu.CompilerParams(dimension_semantics=("arbitrary",)),
    )(lag_blocks[0], block_count, wpad, refrows, a_c, a_s, b_c, b_s)
    return out[None]


def solution(mesh):
    placed = (
        P("beam", None, None, "seg"),
        P("beam", None, None, "seg"),
        P(),
        P("beam"),
        P("beam", None),
        P("beam"),
    )
    return jax.shard_map(
        shards,
        mesh=mesh,
        in_specs=placed,
        out_specs=P("beam", None, None, None, "seg"),
        check_vma=False,
    )
```

```python
import functools
import math

import jax
import jax.numpy as jnp
from jax import lax
from jax.experimental import pallas as pl
from jax.experimental.pallas import tpu as pltpu
from jax.sharding import PartitionSpec as P

LB = 128
NLB = 8
DOP = 256
CHUNK = 2048
PIECE = 1024


def phase_rows(freqs, times, window_len):
    turns = jnp.mod(freqs[:, None] * times[None, :], window_len)
    angle = turns.astype(jnp.float32) * (2.0 * math.pi / window_len)
    return jnp.cos(angle), jnp.sin(angle)


def reverse_rows(x):
    n = x.shape[0]
    rows = lax.broadcasted_iota(jnp.int32, (n, n), 0)
    cols = lax.broadcasted_iota(jnp.int32, (n, n), 1)
    flip = jnp.where(rows + cols == n - 1, 1.0, 0.0).astype(jnp.bfloat16)
    high = x.astype(jnp.bfloat16)
    rest = x - high.astype(jnp.float32)
    mid = rest.astype(jnp.bfloat16)
    low = (rest - mid.astype(jnp.float32)).astype(jnp.bfloat16)
    turn = lambda piece: jnp.dot(flip, piece, preferred_element_type=jnp.float32)
    return (turn(high) + turn(mid)) + turn(low)


def caf_kernel(blocks_ref, count_ref, wpad_ref, ref_ref, ac_ref, as_ref, bc_ref, bs_ref,
               out_ref, first_buf, second_buf, acc, *, chunks, slots, span, steps, norm):
    pair = pl.program_id(0)
    lanes = PIECE + LB
    pieces = [(comp, i) for comp in range(2) for i in range(span // PIECE)]
    share = -(-len(pieces) // chunks)

    def build_piece(step, comp, i, dst):
        v0 = i * PIECE
        win = wpad_ref[step, comp:comp + 1, v0:v0 + lanes]
        tile = jnp.broadcast_to(win, (LB, lanes))
        rolled = pltpu.roll(tile, lanes - LB + 1, 1, stride=1, stride_axis=0)
        dst[comp * LB:(comp + 1) * LB, v0:v0 + PIECE] = rolled[:, :PIECE].astype(jnp.bfloat16)

    @pl.when(pair == 0)
    def _():
        acc[...] = jnp.zeros_like(acc)
        for comp, i in pieces:
            build_piece(0, comp, i, first_buf)

    offsets = [jnp.maximum(blocks_ref[q], 0) * LB for q in range(slots)]

    def one_step(step, cur, nxt, next_step):
        for c in range(chunks):
            g = step * chunks + c
            rr = ref_ref[g]
            r_re = rr[0:1, :]
            r_im = rr[1:2, :]
            a_c = jnp.concatenate([ac_ref[g]] * (CHUNK // LB), axis=1)
            a_s = jnp.concatenate([as_ref[g]] * (CHUNK // LB), axis=1)
            b_c = bc_ref[...]
            b_s = bs_ref[...]
            cos_part = a_c * b_c - a_s * b_s
            sine_part = a_s * b_c + a_c * b_s
            c_re = (r_re * cos_part - r_im * sine_part).astype(jnp.bfloat16)
            c_im = (0.0 - (r_re * sine_part + r_im * cos_part)).astype(jnp.bfloat16)
            coef = jnp.concatenate([c_re, c_im], axis=0)
            for q in range(slots):
                off = pl.multiple_of(offsets[q] + c * CHUNK, LB)
                hank = cur[:, pl.ds(off, CHUNK)]
                acc[q] += lax.dot_general(hank, coef, (((1,), (1,)), ((), ())),
                                          preferred_element_type=jnp.float32)
            for comp, i in pieces[c * share:(c + 1) * share]:
                build_piece(next_step, comp, i, nxt)

    step = 2 * pair
    one_step(step, first_buf, second_buf, step + 1)
    one_step(step + 1, second_buf, first_buf, jnp.minimum(step + 2, steps - 1))

    @pl.when(pair == pl.num_programs(0) - 1)
    def _():
        count = count_ref[0]
        for q in range(slots):
            part = acc[q]
            re = part[:LB, :LB] - part[LB:, LB:]
            im = part[:LB, LB:] + part[LB:, :LB]
            keep = q < count
            out_ref[q, 0] = jnp.where(keep, reverse_rows(re) * norm, 0.0)
            out_ref[q, 1] = jnp.where(keep, reverse_rows(im) * norm, 0.0)


def butterfly_sum(value, axes):
    count = lax.axis_size(axes)
    if count & (count - 1):
        return lax.psum(value, axes)
    stride = 1
    while stride < count:
        radix = 4 if stride * 4 <= count else 2
        parts = [lax.ppermute(value, axes, [(i, i ^ (m * stride)) for i in range(count)]) for m in range(1, radix)]
        for part in parts:
            value = value + part
        stride *= radix
    return value


def seg_join(half, axis):
    count = lax.axis_size(axis)
    parts = lax.all_gather(half, axis, axis=half.ndim - 1, tiled=True) if count != 2 else None
    if parts is not None:
        return parts
    other = lax.ppermute(half, axis, [(0, 1), (1, 0)])
    first = lax.axis_index(axis) == 0
    return jnp.where(first, jnp.concatenate([half, other], -1), jnp.concatenate([other, half], -1))


def shards(surveillance, reference_blocks, owner_index, doppler_start, lag_blocks, block_count):
    segments = lax.axis_size("seg")
    seg_place = lax.axis_index("seg")
    beam_place = lax.axis_index("beam")
    seg_len = surveillance.shape[3]
    step_count = surveillance.shape[2]
    step_len = seg_len * segments
    window_len = step_count * step_len
    slot_count = lag_blocks.shape[1]
    rim_len = NLB * LB
    bins = DOP // segments
    chunks = step_len // CHUNK

    samples = seg_join(surveillance[0], "seg")
    mine = (owner_index == beam_place)[None, :, None]
    local = jnp.where(mine, reference_blocks[0], jnp.zeros_like(reference_blocks[0]))
    if segments == 2:
        first = seg_place == 0
        zero = jnp.zeros_like(local)
        placed = jnp.where(first, jnp.concatenate([local, zero], -1), jnp.concatenate([zero, local], -1))
        refs = butterfly_sum(placed, ("beam", "seg"))
    else:
        refs = seg_join(butterfly_sum(local, "beam"), "seg")

    span = step_len + rim_len
    wpad = jnp.transpose(samples, (1, 0, 2)).astype(jnp.float32)
    wpad = jnp.pad(wpad, ((0, 0), (0, 0), (0, span + LB - step_len)))
    refrows = jnp.transpose(refs.reshape(2, step_count * chunks, CHUNK), (1, 0, 2)).astype(jnp.float32)

    freqs = doppler_start[0] + seg_place * bins + jnp.arange(bins, dtype=jnp.int32)
    a_c, a_s = phase_rows(freqs, jnp.arange(step_count * chunks, dtype=jnp.int32) * CHUNK, window_len)
    h_c, h_s = phase_rows(freqs, jnp.arange(CHUNK // LB, dtype=jnp.int32) * LB, window_len)
    l_c, l_s = phase_rows(freqs, jnp.arange(LB, dtype=jnp.int32), window_len)
    a_c, a_s, h_c, h_s, l_c, l_s = lax.optimization_barrier((a_c, a_s, h_c, h_s, l_c, l_s))
    b_c = jnp.concatenate([h_c[:, i:i + 1] * l_c - h_s[:, i:i + 1] * l_s for i in range(CHUNK // LB)], axis=1)
    b_s = jnp.concatenate([h_s[:, i:i + 1] * l_c + h_c[:, i:i + 1] * l_s for i in range(CHUNK // LB)], axis=1)
    a_c = jnp.broadcast_to(a_c.T[:, :, None], (step_count * chunks, bins, LB))
    a_s = jnp.broadcast_to(a_s.T[:, :, None], (step_count * chunks, bins, LB))

    assert step_count % 2 == 0
    kernel = functools.partial(caf_kernel, chunks=chunks, slots=slot_count, span=span, steps=step_count,
                               norm=1.0 / math.sqrt(window_len))
    full = lambda shape: pl.BlockSpec(shape, lambda k, *_: (0,) * len(shape))
    out = pl.pallas_call(
        kernel,
        out_shape=jax.ShapeDtypeStruct((slot_count, 2, LB, bins), jnp.float32),
        grid_spec=pltpu.PrefetchScalarGridSpec(
            num_scalar_prefetch=2,
            grid=(step_count // 2,),
            in_specs=[full(wpad.shape), full(refrows.shape), full(a_c.shape), full(a_s.shape),
                      full(b_c.shape), full(b_s.shape)],
            out_specs=full((slot_count, 2, LB, bins)),
            scratch_shapes=[pltpu.VMEM((2 * LB, span), jnp.bfloat16), pltpu.VMEM((2 * LB, span), jnp.bfloat16),
                            pltpu.VMEM((slot_count, 2 * LB, 2 * bins), jnp.float32)],
        ),
        compiler_params=pltpu.CompilerParams(dimension_semantics=("arbitrary",)),
    )(lag_blocks[0], block_count, wpad, refrows, a_c, a_s, b_c, b_s)
    return out[None]


def solution(mesh):
    placed = (
        P("beam", None, None, "seg"),
        P("beam", None, None, "seg"),
        P(),
        P("beam"),
        P("beam", None),
        P("beam"),
    )
    return jax.shard_map(
        shards,
        mesh=mesh,
        in_specs=placed,
        out_specs=P("beam", None, None, None, "seg"),
        check_vma=False,
    )
```

```python
import functools
import math

import jax
import jax.numpy as jnp
from jax import lax
from jax.experimental import pallas as pl
from jax.experimental.pallas import tpu as pltpu
from jax.sharding import PartitionSpec as P

LB = 128
NLB = 8
DOP = 256
CHUNK = 2048
PIECE = 1024


def phase_rows(freqs, times, window_len):
    turns = jnp.mod(freqs[:, None] * times[None, :], window_len)
    angle = turns.astype(jnp.float32) * (2.0 * math.pi / window_len)
    return jnp.cos(angle), jnp.sin(angle)


def reverse_rows(x):
    n = x.shape[0]
    rows = lax.broadcasted_iota(jnp.int32, (n, n), 0)
    cols = lax.broadcasted_iota(jnp.int32, (n, n), 1)
    flip = jnp.where(rows + cols == n - 1, 1.0, 0.0).astype(jnp.bfloat16)
    high = x.astype(jnp.bfloat16)
    rest = x - high.astype(jnp.float32)
    mid = rest.astype(jnp.bfloat16)
    low = (rest - mid.astype(jnp.float32)).astype(jnp.bfloat16)
    turn = lambda piece: jnp.dot(flip, piece, preferred_element_type=jnp.float32)
    return (turn(high) + turn(mid)) + turn(low)


def caf_kernel(blocks_ref, count_ref, wpad_ref, ref_ref, ac_ref, as_ref, hc_ref, hs_ref, lc_ref, ls_ref,
               out_ref, first_buf, second_buf, acc, bc_ref, bs_ref, *, chunks, slots, span, steps, norm):
    pair = pl.program_id(0)
    lanes = PIECE + LB
    pieces = [(comp, i) for comp in range(2) for i in range(span // PIECE)]
    share = -(-len(pieces) // chunks)

    def build_piece(step, comp, i, dst):
        v0 = i * PIECE
        win = wpad_ref[step, comp:comp + 1, v0:v0 + lanes]
        tile = jnp.broadcast_to(win, (LB, lanes))
        rolled = pltpu.roll(tile, lanes - LB + 1, 1, stride=1, stride_axis=0)
        dst[comp * LB:(comp + 1) * LB, v0:v0 + PIECE] = rolled[:, :PIECE].astype(jnp.bfloat16)

    @pl.when(pair == 0)
    def _():
        acc[...] = jnp.zeros_like(acc)
        l_c = lc_ref[...]
        l_s = ls_ref[...]
        for i in range(CHUNK // LB):
            h_c = jnp.broadcast_to(hc_ref[:, i:i + 1], (LB, LB))
            h_s = jnp.broadcast_to(hs_ref[:, i:i + 1], (LB, LB))
            bc_ref[:, i * LB:(i + 1) * LB] = h_c * l_c - h_s * l_s
            bs_ref[:, i * LB:(i + 1) * LB] = h_s * l_c + h_c * l_s
        for comp, i in pieces:
            build_piece(0, comp, i, first_buf)

    offsets = [jnp.maximum(blocks_ref[q], 0) * LB for q in range(slots)]

    def one_step(step, cur, nxt, next_step):
        for c in range(chunks):
            g = step * chunks + c
            rr = ref_ref[g]
            r_re = rr[0:1, :]
            r_im = rr[1:2, :]
            pick = lax.broadcasted_iota(jnp.int32, ac_ref.shape, 1) == g
            a_c = jnp.broadcast_to(jnp.sum(jnp.where(pick, ac_ref[...], 0.0), axis=1, keepdims=True), (LB, CHUNK))
            a_s = jnp.broadcast_to(jnp.sum(jnp.where(pick, as_ref[...], 0.0), axis=1, keepdims=True), (LB, CHUNK))
            b_c = bc_ref[...]
            b_s = bs_ref[...]
            cos_part = a_c * b_c - a_s * b_s
            sine_part = a_s * b_c + a_c * b_s
            c_re = (r_re * cos_part - r_im * sine_part).astype(jnp.bfloat16)
            c_im = (0.0 - (r_re * sine_part + r_im * cos_part)).astype(jnp.bfloat16)
            coef = jnp.concatenate([c_re, c_im], axis=0)
            for q in range(slots):
                off = pl.multiple_of(offsets[q] + c * CHUNK, LB)
                hank = cur[:, pl.ds(off, CHUNK)]
                acc[q] += lax.dot_general(hank, coef, (((1,), (1,)), ((), ())),
                                          preferred_element_type=jnp.float32)
            for comp, i in pieces[c * share:(c + 1) * share]:
                build_piece(next_step, comp, i, nxt)

    step = 2 * pair
    one_step(step, first_buf, second_buf, step + 1)
    one_step(step + 1, second_buf, first_buf, jnp.minimum(step + 2, steps - 1))

    @pl.when(pair == pl.num_programs(0) - 1)
    def _():
        count = count_ref[0]
        for q in range(slots):
            part = acc[q]
            re = part[:LB, :LB] - part[LB:, LB:]
            im = part[:LB, LB:] + part[LB:, :LB]
            keep = q < count
            out_ref[q, 0] = jnp.where(keep, reverse_rows(re) * norm, 0.0)
            out_ref[q, 1] = jnp.where(keep, reverse_rows(im) * norm, 0.0)


def butterfly_sum(value, axes):
    count = lax.axis_size(axes)
    if count & (count - 1):
        return lax.psum(value, axes)
    stride = 1
    while stride < count:
        radix = 4 if stride * 4 <= count else 2
        parts = [lax.ppermute(value, axes, [(i, i ^ (m * stride)) for i in range(count)]) for m in range(1, radix)]
        for part in parts:
            value = value + part
        stride *= radix
    return value


def seg_join(half, axis):
    count = lax.axis_size(axis)
    parts = lax.all_gather(half, axis, axis=half.ndim - 1, tiled=True) if count != 2 else None
    if parts is not None:
        return parts
    other = lax.ppermute(half, axis, [(0, 1), (1, 0)])
    first = lax.axis_index(axis) == 0
    return jnp.where(first, jnp.concatenate([half, other], -1), jnp.concatenate([other, half], -1))


def shards(surveillance, reference_blocks, owner_index, doppler_start, lag_blocks, block_count):
    segments = lax.axis_size("seg")
    seg_place = lax.axis_index("seg")
    beam_place = lax.axis_index("beam")
    seg_len = surveillance.shape[3]
    step_count = surveillance.shape[2]
    step_len = seg_len * segments
    window_len = step_count * step_len
    slot_count = lag_blocks.shape[1]
    rim_len = NLB * LB
    bins = DOP // segments
    chunks = step_len // CHUNK

    samples = seg_join(surveillance[0], "seg")
    mine = (owner_index == beam_place)[None, :, None]
    local = jnp.where(mine, reference_blocks[0], jnp.zeros_like(reference_blocks[0]))
    if segments == 2:
        first = seg_place == 0
        zero = jnp.zeros_like(local)
        placed = jnp.where(first, jnp.concatenate([local, zero], -1), jnp.concatenate([zero, local], -1))
        refs = butterfly_sum(placed, ("beam", "seg"))
    else:
        refs = seg_join(butterfly_sum(local, "beam"), "seg")

    span = step_len + rim_len
    wpad = jnp.transpose(samples, (1, 0, 2)).astype(jnp.float32)
    wpad = jnp.pad(wpad, ((0, 0), (0, 0), (0, span + LB - step_len)))
    refrows = jnp.transpose(refs.reshape(2, step_count * chunks, CHUNK), (1, 0, 2)).astype(jnp.float32)

    freqs = doppler_start[0] + seg_place * bins + jnp.arange(bins, dtype=jnp.int32)
    a_c, a_s = phase_rows(freqs, jnp.arange(step_count * chunks, dtype=jnp.int32) * CHUNK, window_len)
    h_c, h_s = phase_rows(freqs, jnp.arange(CHUNK // LB, dtype=jnp.int32) * LB, window_len)
    l_c, l_s = phase_rows(freqs, jnp.arange(LB, dtype=jnp.int32), window_len)

    tables = (a_c, a_s, h_c, h_s, l_c, l_s)
    assert step_count % 2 == 0
    kernel = functools.partial(caf_kernel, chunks=chunks, slots=slot_count, span=span, steps=step_count,
                               norm=1.0 / math.sqrt(window_len))
    full = lambda shape: pl.BlockSpec(shape, lambda k, *_: (0,) * len(shape))
    out = pl.pallas_call(
        kernel,
        out_shape=jax.ShapeDtypeStruct((slot_count, 2, LB, bins), jnp.float32),
        grid_spec=pltpu.PrefetchScalarGridSpec(
            num_scalar_prefetch=2,
            grid=(step_count // 2,),
            in_specs=[full(wpad.shape), full(refrows.shape)] + [full(t.shape) for t in tables],
            out_specs=full((slot_count, 2, LB, bins)),
            scratch_shapes=[pltpu.VMEM((2 * LB, span), jnp.bfloat16), pltpu.VMEM((2 * LB, span), jnp.bfloat16),
                            pltpu.VMEM((slot_count, 2 * LB, 2 * bins), jnp.float32),
                            pltpu.VMEM((bins, CHUNK), jnp.float32), pltpu.VMEM((bins, CHUNK), jnp.float32)],
        ),
        compiler_params=pltpu.CompilerParams(dimension_semantics=("arbitrary",)),
    )(lag_blocks[0], block_count, wpad, refrows, *tables)
    return out[None]


def solution(mesh):
    placed = (
        P("beam", None, None, "seg"),
        P("beam", None, None, "seg"),
        P(),
        P("beam"),
        P("beam", None),
        P("beam"),
    )
    return jax.shard_map(
        shards,
        mesh=mesh,
        in_specs=placed,
        out_specs=P("beam", None, None, None, "seg"),
        check_vma=False,
    )
```

```python
import functools
import math

import jax
import jax.numpy as jnp
from jax import lax
from jax.experimental import pallas as pl
from jax.experimental.pallas import tpu as pltpu
from jax.sharding import PartitionSpec as P

LB = 128
NLB = 8
DOP = 256
CHUNK = 2048
PIECE = 1024


def phase_rows(freqs, times, window_len):
    turns = jnp.mod(freqs[:, None] * times[None, :], window_len)
    angle = turns.astype(jnp.float32) * (2.0 * math.pi / window_len)
    return jnp.cos(angle), jnp.sin(angle)


def reverse_rows(x):
    n = x.shape[0]
    rows = lax.broadcasted_iota(jnp.int32, (n, n), 0)
    cols = lax.broadcasted_iota(jnp.int32, (n, n), 1)
    flip = jnp.where(rows + cols == n - 1, 1.0, 0.0).astype(jnp.bfloat16)
    high = x.astype(jnp.bfloat16)
    rest = x - high.astype(jnp.float32)
    mid = rest.astype(jnp.bfloat16)
    low = (rest - mid.astype(jnp.float32)).astype(jnp.bfloat16)
    turn = lambda piece: jnp.dot(flip, piece, preferred_element_type=jnp.float32)
    return (turn(high) + turn(mid)) + turn(low)


def caf_kernel(blocks_ref, count_ref, wpad_ref, ref_ref, ac_ref, as_ref, hc_ref, hs_ref, lc_ref, ls_ref,
               out_ref, first_buf, second_buf, acc, bc_ref, bs_ref, *, chunks, slots, span, steps, norm):
    pair = pl.program_id(0)
    lanes = PIECE + LB
    pieces = [(comp, i) for comp in range(2) for i in range(span // PIECE)]
    share = -(-len(pieces) // chunks)

    def build_piece(step, comp, i, dst):
        v0 = i * PIECE
        win = wpad_ref[step, comp:comp + 1, v0:v0 + lanes]
        tile = jnp.broadcast_to(win, (LB, lanes))
        rolled = pltpu.roll(tile, lanes - LB + 1, 1, stride=1, stride_axis=0)
        dst[comp * LB:(comp + 1) * LB, v0:v0 + PIECE] = rolled[:, :PIECE].astype(jnp.bfloat16)

    @pl.when(pair == 0)
    def _():
        acc[...] = jnp.zeros_like(acc)
        l_c = lc_ref[...]
        l_s = ls_ref[...]
        for i in range(CHUNK // LB):
            h_c = jnp.broadcast_to(hc_ref[:, i:i + 1], (LB, LB))
            h_s = jnp.broadcast_to(hs_ref[:, i:i + 1], (LB, LB))
            bc_ref[:, i * LB:(i + 1) * LB] = h_c * l_c - h_s * l_s
            bs_ref[:, i * LB:(i + 1) * LB] = h_s * l_c + h_c * l_s
        for comp, i in pieces:
            build_piece(0, comp, i, first_buf)

    offsets = [jnp.maximum(blocks_ref[q], 0) * LB for q in range(slots)]

    def one_step(step, cur, nxt, next_step):
        for c in range(chunks):
            g = step * chunks + c
            rr = ref_ref[g]
            r_re = rr[0:1, :]
            r_im = rr[1:2, :]
            pick = lax.broadcasted_iota(jnp.int32, ac_ref.shape, 1) == g
            a_c = jnp.broadcast_to(jnp.sum(jnp.where(pick, ac_ref[...], 0.0), axis=1, keepdims=True), (LB, CHUNK))
            a_s = jnp.broadcast_to(jnp.sum(jnp.where(pick, as_ref[...], 0.0), axis=1, keepdims=True), (LB, CHUNK))
            b_c = bc_ref[...]
            b_s = bs_ref[...]
            cos_part = a_c * b_c - a_s * b_s
            sine_part = a_s * b_c + a_c * b_s
            c_re = (r_re * cos_part - r_im * sine_part).astype(jnp.bfloat16)
            c_im = (0.0 - (r_re * sine_part + r_im * cos_part)).astype(jnp.bfloat16)
            coef = jnp.concatenate([c_re, c_im], axis=0)
            for q in range(slots):
                off = pl.multiple_of(offsets[q] + c * CHUNK, LB)
                hank = cur[:, pl.ds(off, CHUNK)]
                acc[q] += lax.dot_general(hank, coef, (((1,), (1,)), ((), ())),
                                          preferred_element_type=jnp.float32)
            for comp, i in pieces[c * share:(c + 1) * share]:
                build_piece(next_step, comp, i, nxt)

    step = 2 * pair
    one_step(step, first_buf, second_buf, step + 1)
    one_step(step + 1, second_buf, first_buf, jnp.minimum(step + 2, steps - 1))

    @pl.when(pair == pl.num_programs(0) - 1)
    def _():
        count = count_ref[0]
        for q in range(slots):
            part = acc[q]
            re = part[:LB, :LB] - part[LB:, LB:]
            im = part[:LB, LB:] + part[LB:, :LB]
            keep = q < count
            out_ref[q, 0] = jnp.where(keep, reverse_rows(re) * norm, 0.0)
            out_ref[q, 1] = jnp.where(keep, reverse_rows(im) * norm, 0.0)


def butterfly_sum(value, axes, later=()):
    count = lax.axis_size(axes)
    if count & (count - 1):
        return lax.psum(value, axes), later
    stride = 1
    while stride < count:
        radix = 4 if stride * 4 <= count else 2
        parts = [lax.ppermute(value, axes, [(i, i ^ (m * stride)) for i in range(count)]) for m in range(1, radix)]
        for part in parts:
            value = value + part
        if stride == 1:
            late = (value.reshape(-1)[0] != value.reshape(-1)[0]).astype(jnp.int32)
            later = jax.tree.map(lambda x: x + late.astype(x.dtype), later)
        stride *= radix
    return value, later


def seg_join(half, axis):
    count = lax.axis_size(axis)
    parts = lax.all_gather(half, axis, axis=half.ndim - 1, tiled=True) if count != 2 else None
    if parts is not None:
        return parts
    other = lax.ppermute(half, axis, [(0, 1), (1, 0)])
    first = lax.axis_index(axis) == 0
    return jnp.where(first, jnp.concatenate([half, other], -1), jnp.concatenate([other, half], -1))


def shards(surveillance, reference_blocks, owner_index, doppler_start, lag_blocks, block_count):
    segments = lax.axis_size("seg")
    seg_place = lax.axis_index("seg")
    beam_place = lax.axis_index("beam")
    seg_len = surveillance.shape[3]
    step_count = surveillance.shape[2]
    step_len = seg_len * segments
    window_len = step_count * step_len
    slot_count = lag_blocks.shape[1]
    rim_len = NLB * LB
    bins = DOP // segments
    chunks = step_len // CHUNK

    mine = (owner_index == beam_place)[None, :, None]
    local = jnp.where(mine, reference_blocks[0], jnp.zeros_like(reference_blocks[0]))
    if segments == 2:
        first = seg_place == 0
        zero = jnp.zeros_like(local)
        placed = jnp.where(first, jnp.concatenate([local, zero], -1), jnp.concatenate([zero, local], -1))
        refs, (own_samples, first_bin) = butterfly_sum(placed, ("beam", "seg"), (surveillance[0], doppler_start[0]))
    else:
        refs, (own_samples, first_bin) = butterfly_sum(local, "beam", (surveillance[0], doppler_start[0]))
        refs = seg_join(refs, "seg")
    samples = seg_join(own_samples, "seg")

    span = step_len + rim_len
    wpad = jnp.transpose(samples, (1, 0, 2)).astype(jnp.float32)
    wpad = jnp.pad(wpad, ((0, 0), (0, 0), (0, span + LB - step_len)))
    refrows = jnp.transpose(refs.reshape(2, step_count * chunks, CHUNK), (1, 0, 2)).astype(jnp.float32)

    freqs = first_bin + seg_place * bins + jnp.arange(bins, dtype=jnp.int32)
    a_c, a_s = phase_rows(freqs, jnp.arange(step_count * chunks, dtype=jnp.int32) * CHUNK, window_len)
    h_c, h_s = phase_rows(freqs, jnp.arange(CHUNK // LB, dtype=jnp.int32) * LB, window_len)
    l_c, l_s = phase_rows(freqs, jnp.arange(LB, dtype=jnp.int32), window_len)

    tables = (a_c, a_s, h_c, h_s, l_c, l_s)
    assert step_count % 2 == 0
    kernel = functools.partial(caf_kernel, chunks=chunks, slots=slot_count, span=span, steps=step_count,
                               norm=1.0 / math.sqrt(window_len))
    full = lambda shape: pl.BlockSpec(shape, lambda k, *_: (0,) * len(shape))
    out = pl.pallas_call(
        kernel,
        out_shape=jax.ShapeDtypeStruct((slot_count, 2, LB, bins), jnp.float32),
        grid_spec=pltpu.PrefetchScalarGridSpec(
            num_scalar_prefetch=2,
            grid=(step_count // 2,),
            in_specs=[full(wpad.shape), full(refrows.shape)] + [full(t.shape) for t in tables],
            out_specs=full((slot_count, 2, LB, bins)),
            scratch_shapes=[pltpu.VMEM((2 * LB, span), jnp.bfloat16), pltpu.VMEM((2 * LB, span), jnp.bfloat16),
                            pltpu.VMEM((slot_count, 2 * LB, 2 * bins), jnp.float32),
                            pltpu.VMEM((bins, CHUNK), jnp.float32), pltpu.VMEM((bins, CHUNK), jnp.float32)],
        ),
        compiler_params=pltpu.CompilerParams(dimension_semantics=("arbitrary",)),
    )(lag_blocks[0], block_count, wpad, refrows, *tables)
    return out[None]


def solution(mesh):
    placed = (
        P("beam", None, None, "seg"),
        P("beam", None, None, "seg"),
        P(),
        P("beam"),
        P("beam", None),
        P("beam"),
    )
    return jax.shard_map(
        shards,
        mesh=mesh,
        in_specs=placed,
        out_specs=P("beam", None, None, None, "seg"),
        check_vma=False,
    )
```

```python
import functools
import math

import jax
import jax.numpy as jnp
from jax import lax
from jax.experimental import pallas as pl
from jax.experimental.pallas import tpu as pltpu
from jax.sharding import PartitionSpec as P

LB = 128
NLB = 8
DOP = 256
CHUNK = 2048
PIECE = 1024


def phase_rows(freqs, times, window_len):
    turns = jnp.mod(freqs[:, None] * times[None, :], window_len)
    angle = turns.astype(jnp.float32) * (2.0 * math.pi / window_len)
    return jnp.cos(angle), jnp.sin(angle)


def reverse_rows(x):
    n = x.shape[0]
    rows = lax.broadcasted_iota(jnp.int32, (n, n), 0)
    cols = lax.broadcasted_iota(jnp.int32, (n, n), 1)
    flip = jnp.where(rows + cols == n - 1, 1.0, 0.0).astype(jnp.bfloat16)
    high = x.astype(jnp.bfloat16)
    rest = x - high.astype(jnp.float32)
    mid = rest.astype(jnp.bfloat16)
    low = (rest - mid.astype(jnp.float32)).astype(jnp.bfloat16)
    turn = lambda piece: jnp.dot(flip, piece, preferred_element_type=jnp.float32)
    return (turn(high) + turn(mid)) + turn(low)


def caf_kernel(blocks_ref, count_ref, wpad_ref, ref_ref, cos_ref, sin_ref,
               out_ref, first_buf, second_buf, acc, bc_ref, bs_ref, *, chunks, slots, span, steps, groups, norm):
    def column(ref, lane):
        tail = ref[:, LB:]
        pick = lax.broadcasted_iota(jnp.int32, tail.shape, 1) == lane
        return jnp.sum(jnp.where(pick, tail, 0.0), axis=1, keepdims=True)

    pair = pl.program_id(0)
    lanes = PIECE + LB
    pieces = [(comp, i) for comp in range(2) for i in range(span // PIECE)]
    share = -(-len(pieces) // chunks)

    def build_piece(step, comp, i, dst):
        v0 = i * PIECE
        win = wpad_ref[step, comp:comp + 1, v0:v0 + lanes]
        tile = jnp.broadcast_to(win, (LB, lanes))
        rolled = pltpu.roll(tile, lanes - LB + 1, 1, stride=1, stride_axis=0)
        dst[comp * LB:(comp + 1) * LB, v0:v0 + PIECE] = rolled[:, :PIECE].astype(jnp.bfloat16)

    @pl.when(pair == 0)
    def _():
        acc[...] = jnp.zeros_like(acc)
        l_c = cos_ref[:, :LB]
        l_s = sin_ref[:, :LB]
        for i in range(CHUNK // LB):
            h_c = jnp.broadcast_to(column(cos_ref, groups + i), (LB, LB))
            h_s = jnp.broadcast_to(column(sin_ref, groups + i), (LB, LB))
            bc_ref[:, i * LB:(i + 1) * LB] = h_c * l_c - h_s * l_s
            bs_ref[:, i * LB:(i + 1) * LB] = h_s * l_c + h_c * l_s
        for comp, i in pieces:
            build_piece(0, comp, i, first_buf)

    offsets = [jnp.maximum(blocks_ref[q], 0) * LB for q in range(slots)]

    def one_step(step, cur, nxt, next_step):
        for c in range(chunks):
            g = step * chunks + c
            rr = ref_ref[g]
            r_re = rr[0:1, :]
            r_im = rr[1:2, :]
            a_c = jnp.broadcast_to(column(cos_ref, g), (LB, CHUNK))
            a_s = jnp.broadcast_to(column(sin_ref, g), (LB, CHUNK))
            b_c = bc_ref[...]
            b_s = bs_ref[...]
            cos_part = a_c * b_c - a_s * b_s
            sine_part = a_s * b_c + a_c * b_s
            c_re = (r_re * cos_part - r_im * sine_part).astype(jnp.bfloat16)
            c_im = (0.0 - (r_re * sine_part + r_im * cos_part)).astype(jnp.bfloat16)
            coef = jnp.concatenate([c_re, c_im], axis=0)
            for q in range(slots):
                off = pl.multiple_of(offsets[q] + c * CHUNK, LB)
                hank = cur[:, pl.ds(off, CHUNK)]
                acc[q] += lax.dot_general(hank, coef, (((1,), (1,)), ((), ())),
                                          preferred_element_type=jnp.float32)
            for comp, i in pieces[c * share:(c + 1) * share]:
                build_piece(next_step, comp, i, nxt)

    step = 2 * pair
    one_step(step, first_buf, second_buf, step + 1)
    one_step(step + 1, second_buf, first_buf, jnp.minimum(step + 2, steps - 1))

    @pl.when(pair == pl.num_programs(0) - 1)
    def _():
        count = count_ref[0]
        for q in range(slots):
            part = acc[q]
            re = part[:LB, :LB] - part[LB:, LB:]
            im = part[:LB, LB:] + part[LB:, :LB]
            keep = q < count
            out_ref[q, 0] = jnp.where(keep, reverse_rows(re) * norm, 0.0)
            out_ref[q, 1] = jnp.where(keep, reverse_rows(im) * norm, 0.0)


def butterfly_sum(value, axes, later=(), rider=None):
    count = lax.axis_size(axes)
    stride = 1
    carried = None
    while stride < count:
        radix = 4 if stride * 4 <= count else 2
        parts = []
        for m in range(1, radix):
            pairs = [(i, i ^ (m * stride)) for i in range(count)]
            if stride == 1 and m == 1 and rider is not None:
                both = lax.ppermute(jnp.concatenate([value, rider], -1), axes, pairs)
                parts.append(both[..., :value.shape[-1]])
                carried = both[..., value.shape[-1]:]
            else:
                parts.append(lax.ppermute(value, axes, pairs))
        for part in parts:
            value = value + part
        if stride == 1:
            late = (value.reshape(-1)[0] != value.reshape(-1)[0]).astype(jnp.int32)
            later = jax.tree.map(lambda x: x + late.astype(x.dtype), later)
        stride *= radix
    return value, later, carried


def seg_join(half, axis):
    count = lax.axis_size(axis)
    parts = lax.all_gather(half, axis, axis=half.ndim - 1, tiled=True) if count != 2 else None
    if parts is not None:
        return parts
    other = lax.ppermute(half, axis, [(0, 1), (1, 0)])
    first = lax.axis_index(axis) == 0
    return jnp.where(first, jnp.concatenate([half, other], -1), jnp.concatenate([other, half], -1))


def shards(surveillance, reference_blocks, owner_index, doppler_start, lag_blocks, block_count):
    segments = lax.axis_size("seg")
    seg_place = lax.axis_index("seg")
    beam_place = lax.axis_index("beam")
    seg_len = surveillance.shape[3]
    step_count = surveillance.shape[2]
    step_len = seg_len * segments
    window_len = step_count * step_len
    slot_count = lag_blocks.shape[1]
    rim_len = NLB * LB
    bins = DOP // segments
    chunks = step_len // CHUNK

    mine = (owner_index == beam_place)[None, :, None]
    local = jnp.where(mine, reference_blocks[0], jnp.zeros_like(reference_blocks[0]))
    group = lax.axis_size(("beam", "seg"))
    if segments == 2 and group >= 4 and not group & (group - 1):
        first = seg_place == 0
        zero = jnp.zeros_like(local)
        placed = jnp.where(first, jnp.concatenate([local, zero], -1), jnp.concatenate([zero, local], -1))
        refs, (first_bin,), other = butterfly_sum(placed, ("beam", "seg"), (doppler_start[0],), surveillance[0])
        samples = jnp.where(first, jnp.concatenate([surveillance[0], other], -1),
                            jnp.concatenate([other, surveillance[0]], -1))
    else:
        refs = seg_join(lax.psum(local, "beam"), "seg")
        samples = seg_join(surveillance[0], "seg")
        first_bin = doppler_start[0]

    span = step_len + rim_len
    wpad = jnp.transpose(samples, (1, 0, 2)).astype(jnp.float32)
    wpad = jnp.pad(wpad, ((0, 0), (0, 0), (0, span + LB - step_len)))
    refrows = jnp.transpose(refs.reshape(2, step_count * chunks, CHUNK), (1, 0, 2)).astype(jnp.float32)

    freqs = first_bin + seg_place * bins + jnp.arange(bins, dtype=jnp.int32)
    times = jnp.concatenate([jnp.arange(LB, dtype=jnp.int32),
                             jnp.arange(step_count * chunks, dtype=jnp.int32) * CHUNK,
                             jnp.arange(CHUNK // LB, dtype=jnp.int32) * LB])
    cos_rows, sin_rows = phase_rows(freqs, times, window_len)
    tables = (cos_rows, sin_rows)
    assert step_count % 2 == 0
    kernel = functools.partial(caf_kernel, chunks=chunks, slots=slot_count, span=span, steps=step_count,
                               groups=step_count * chunks,
                               norm=1.0 / math.sqrt(window_len))
    full = lambda shape: pl.BlockSpec(shape, lambda k, *_: (0,) * len(shape))
    out = pl.pallas_call(
        kernel,
        out_shape=jax.ShapeDtypeStruct((slot_count, 2, LB, bins), jnp.float32),
        grid_spec=pltpu.PrefetchScalarGridSpec(
            num_scalar_prefetch=2,
            grid=(step_count // 2,),
            in_specs=[full(wpad.shape), full(refrows.shape)] + [full(t.shape) for t in tables],
            out_specs=full((slot_count, 2, LB, bins)),
            scratch_shapes=[pltpu.VMEM((2 * LB, span), jnp.bfloat16), pltpu.VMEM((2 * LB, span), jnp.bfloat16),
                            pltpu.VMEM((slot_count, 2 * LB, 2 * bins), jnp.float32),
                            pltpu.VMEM((bins, CHUNK), jnp.float32), pltpu.VMEM((bins, CHUNK), jnp.float32)],
        ),
        compiler_params=pltpu.CompilerParams(dimension_semantics=("arbitrary",)),
    )(lag_blocks[0], block_count, wpad, refrows, *tables)
    return out[None]


def solution(mesh):
    placed = (
        P("beam", None, None, "seg"),
        P("beam", None, None, "seg"),
        P(),
        P("beam"),
        P("beam", None),
        P("beam"),
    )
    return jax.shard_map(
        shards,
        mesh=mesh,
        in_specs=placed,
        out_specs=P("beam", None, None, None, "seg"),
        check_vma=False,
    )
```

```python
import functools
import math

import jax
import jax.numpy as jnp
from jax import lax
from jax.experimental import pallas as pl
from jax.experimental.pallas import tpu as pltpu
from jax.sharding import PartitionSpec as P

LB = 128
NLB = 8
DOP = 256
CHUNK = 2048
PIECE = 1024


def phase_rows(freqs, times, window_len):
    turns = jnp.mod(freqs[:, None] * times[None, :], window_len)
    angle = turns.astype(jnp.float32) * (2.0 * math.pi / window_len)
    return jnp.cos(angle), jnp.sin(angle)


def reverse_rows(x):
    n = x.shape[0]
    rows = lax.broadcasted_iota(jnp.int32, (n, n), 0)
    cols = lax.broadcasted_iota(jnp.int32, (n, n), 1)
    flip = jnp.where(rows + cols == n - 1, 1.0, 0.0).astype(jnp.bfloat16)
    high = x.astype(jnp.bfloat16)
    rest = x - high.astype(jnp.float32)
    mid = rest.astype(jnp.bfloat16)
    low = (rest - mid.astype(jnp.float32)).astype(jnp.bfloat16)
    turn = lambda piece: jnp.dot(flip, piece, preferred_element_type=jnp.float32)
    return (turn(high) + turn(mid)) + turn(low)


def caf_kernel(blocks_ref, count_ref, wpad_ref, ref_ref, cos_ref, sin_ref,
               out_ref, first_buf, second_buf, acc, bc_ref, bs_ref, *, chunks, slots, span, steps, groups, norm):
    def column(ref, lane):
        tail = ref[:, LB:]
        pick = lax.broadcasted_iota(jnp.int32, tail.shape, 1) == lane
        return jnp.sum(jnp.where(pick, tail, 0.0), axis=1, keepdims=True)

    pair = pl.program_id(0)
    lanes = PIECE + LB
    pieces = [(comp, i) for comp in range(2) for i in range(span // PIECE)]
    share = -(-len(pieces) // chunks)

    def build_piece(step, comp, i, dst):
        v0 = i * PIECE
        win = wpad_ref[step, comp:comp + 1, v0:v0 + lanes]
        tile = jnp.broadcast_to(win, (LB, lanes))
        rolled = pltpu.roll(tile, lanes - LB + 1, 1, stride=1, stride_axis=0)
        dst[comp * LB:(comp + 1) * LB, v0:v0 + PIECE] = rolled[:, :PIECE].astype(jnp.bfloat16)

    @pl.when(pair == 0)
    def _():
        acc[...] = jnp.zeros_like(acc)
        l_c = cos_ref[:, :LB]
        l_s = sin_ref[:, :LB]
        for i in range(CHUNK // LB):
            h_c = jnp.broadcast_to(column(cos_ref, groups + i), (LB, LB))
            h_s = jnp.broadcast_to(column(sin_ref, groups + i), (LB, LB))
            bc_ref[:, i * LB:(i + 1) * LB] = h_c * l_c - h_s * l_s
            bs_ref[:, i * LB:(i + 1) * LB] = h_s * l_c + h_c * l_s
        for comp, i in pieces:
            build_piece(0, comp, i, first_buf)

    offsets = [jnp.maximum(blocks_ref[q], 0) * LB for q in range(slots)]

    def one_step(step, cur, nxt, next_step):
        for c in range(chunks):
            g = step * chunks + c
            rr = ref_ref[g].astype(jnp.float32)
            r_re = rr[0:1, :]
            r_im = rr[1:2, :]
            a_c = jnp.broadcast_to(column(cos_ref, g), (LB, CHUNK))
            a_s = jnp.broadcast_to(column(sin_ref, g), (LB, CHUNK))
            b_c = bc_ref[...]
            b_s = bs_ref[...]
            cos_part = a_c * b_c - a_s * b_s
            sine_part = a_s * b_c + a_c * b_s
            c_re = (r_re * cos_part - r_im * sine_part).astype(jnp.bfloat16)
            c_im = (0.0 - (r_re * sine_part + r_im * cos_part)).astype(jnp.bfloat16)
            coef = jnp.concatenate([c_re, c_im], axis=0)
            for q in range(slots):
                off = pl.multiple_of(offsets[q] + c * CHUNK, LB)
                hank = cur[:, pl.ds(off, CHUNK)]
                acc[q] += lax.dot_general(hank, coef, (((1,), (1,)), ((), ())),
                                          preferred_element_type=jnp.float32)
            for comp, i in pieces[c * share:(c + 1) * share]:
                build_piece(next_step, comp, i, nxt)

    step = 2 * pair
    one_step(step, first_buf, second_buf, step + 1)
    one_step(step + 1, second_buf, first_buf, jnp.minimum(step + 2, steps - 1))

    @pl.when(pair == pl.num_programs(0) - 1)
    def _():
        count = count_ref[0]
        for q in range(slots):
            part = acc[q]
            re = part[:LB, :LB] - part[LB:, LB:]
            im = part[:LB, LB:] + part[LB:, :LB]
            keep = q < count
            out_ref[q, 0] = jnp.where(keep, reverse_rows(re) * norm, 0.0)
            out_ref[q, 1] = jnp.where(keep, reverse_rows(im) * norm, 0.0)


def butterfly_sum(value, axes, later=(), rider=None):
    count = lax.axis_size(axes)
    stride = 1
    carried = None
    while stride < count:
        radix = 4 if stride * 4 <= count else 2
        parts = []
        for m in range(1, radix):
            pairs = [(i, i ^ (m * stride)) for i in range(count)]
            if stride == 1 and m == 1 and rider is not None:
                both = lax.ppermute(jnp.concatenate([value, rider], 0), axes, pairs)
                parts.append(both[:value.shape[0]])
                carried = both[value.shape[0]:]
            else:
                parts.append(lax.ppermute(value, axes, pairs))
        for part in parts:
            value = value + part
        if stride == 1:
            late = (value.reshape(-1)[0] != value.reshape(-1)[0]).astype(jnp.int32)
            later = jax.tree.map(lambda x: x + late.astype(x.dtype), later)
        stride *= radix
    return value, later, carried


def seg_join(half, axis):
    count = lax.axis_size(axis)
    parts = lax.all_gather(half, axis, axis=half.ndim - 1, tiled=True) if count != 2 else None
    if parts is not None:
        return parts
    other = lax.ppermute(half, axis, [(0, 1), (1, 0)])
    first = lax.axis_index(axis) == 0
    return jnp.where(first, jnp.concatenate([half, other], -1), jnp.concatenate([other, half], -1))


def shards(surveillance, reference_blocks, owner_index, doppler_start, lag_blocks, block_count):
    segments = lax.axis_size("seg")
    seg_place = lax.axis_index("seg")
    beam_place = lax.axis_index("beam")
    seg_len = surveillance.shape[3]
    step_count = surveillance.shape[2]
    step_len = seg_len * segments
    window_len = step_count * step_len
    slot_count = lag_blocks.shape[1]
    rim_len = NLB * LB
    bins = DOP // segments
    chunks = step_len // CHUNK

    mine = (owner_index == beam_place)[None, :, None]
    local = jnp.where(mine, reference_blocks[0], jnp.zeros_like(reference_blocks[0]))
    group = lax.axis_size(("beam", "seg"))
    if segments == 2 and group >= 4 and not group & (group - 1) and seg_len == CHUNK:
        first = seg_place == 0
        own = jnp.transpose(local, (1, 0, 2))
        zero = jnp.zeros_like(own)
        placed = jnp.where(first, jnp.stack([own, zero], 1), jnp.stack([zero, own], 1)).reshape(-1, 2, seg_len)
        mine_samples = jnp.transpose(surveillance[0], (1, 0, 2))
        refrows, (first_bin,), other = butterfly_sum(placed, ("beam", "seg"), (doppler_start[0],), mine_samples)
        samples = jnp.where(first, jnp.concatenate([mine_samples, other], -1),
                            jnp.concatenate([other, mine_samples], -1))
    else:
        refs = seg_join(lax.psum(local, "beam"), "seg")
        refrows = jnp.transpose(refs.reshape(2, step_count * chunks, CHUNK), (1, 0, 2))
        samples = jnp.transpose(seg_join(surveillance[0], "seg"), (1, 0, 2))
        first_bin = doppler_start[0]

    span = step_len + rim_len
    wpad = samples.astype(jnp.float32)
    wpad = jnp.pad(wpad, ((0, 0), (0, 0), (0, span + LB - step_len)))

    freqs = first_bin + seg_place * bins + jnp.arange(bins, dtype=jnp.int32)
    times = jnp.concatenate([jnp.arange(LB, dtype=jnp.int32),
                             jnp.arange(step_count * chunks, dtype=jnp.int32) * CHUNK,
                             jnp.arange(CHUNK // LB, dtype=jnp.int32) * LB])
    cos_rows, sin_rows = phase_rows(freqs, times, window_len)
    tables = (cos_rows, sin_rows)
    assert step_count % 2 == 0
    kernel = functools.partial(caf_kernel, chunks=chunks, slots=slot_count, span=span, steps=step_count,
                               groups=step_count * chunks,
                               norm=1.0 / math.sqrt(window_len))
    full = lambda shape: pl.BlockSpec(shape, lambda k, *_: (0,) * len(shape))
    out = pl.pallas_call(
        kernel,
        out_shape=jax.ShapeDtypeStruct((slot_count, 2, LB, bins), jnp.float32),
        grid_spec=pltpu.PrefetchScalarGridSpec(
            num_scalar_prefetch=2,
            grid=(step_count // 2,),
            in_specs=[full(wpad.shape), full(refrows.shape)] + [full(t.shape) for t in tables],
            out_specs=full((slot_count, 2, LB, bins)),
            scratch_shapes=[pltpu.VMEM((2 * LB, span), jnp.bfloat16), pltpu.VMEM((2 * LB, span), jnp.bfloat16),
                            pltpu.VMEM((slot_count, 2 * LB, 2 * bins), jnp.float32),
                            pltpu.VMEM((bins, CHUNK), jnp.float32), pltpu.VMEM((bins, CHUNK), jnp.float32)],
        ),
        compiler_params=pltpu.CompilerParams(dimension_semantics=("arbitrary",)),
    )(lag_blocks[0], block_count, wpad, refrows, *tables)
    return out[None]


def solution(mesh):
    placed = (
        P("beam", None, None, "seg"),
        P("beam", None, None, "seg"),
        P(),
        P("beam"),
        P("beam", None),
        P("beam"),
    )
    return jax.shard_map(
        shards,
        mesh=mesh,
        in_specs=placed,
        out_specs=P("beam", None, None, None, "seg"),
        check_vma=False,
    )
```

```python
import functools
import math

import jax
import jax.numpy as jnp
from jax import lax
from jax.experimental import pallas as pl
from jax.experimental.pallas import tpu as pltpu
from jax.sharding import PartitionSpec as P

LB = 128
NLB = 8
DOP = 256
CHUNK = 2048
PIECE = 1024


def phase_rows(freqs, times, window_len):
    turns = jnp.mod(freqs[:, None] * times[None, :], window_len)
    angle = turns.astype(jnp.float32) * (2.0 * math.pi / window_len)
    return jnp.cos(angle), jnp.sin(angle)


def reverse_rows(x):
    n = x.shape[0]
    rows = lax.broadcasted_iota(jnp.int32, (n, n), 0)
    cols = lax.broadcasted_iota(jnp.int32, (n, n), 1)
    flip = jnp.where(rows + cols == n - 1, 1.0, 0.0).astype(jnp.bfloat16)
    high = x.astype(jnp.bfloat16)
    rest = x - high.astype(jnp.float32)
    mid = rest.astype(jnp.bfloat16)
    low = (rest - mid.astype(jnp.float32)).astype(jnp.bfloat16)
    turn = lambda piece: jnp.dot(flip, piece, preferred_element_type=jnp.float32)
    return (turn(high) + turn(mid)) + turn(low)


def caf_kernel(blocks_ref, count_ref, wpad_ref, cos_ref, sin_ref, *rest, parts, chunks, slots, span, steps,
               groups, norm):
    ref_refs = rest[:parts]
    out_ref, first_buf, second_buf, acc, bc_ref, bs_ref = rest[parts:]
    def column(ref, lane):
        tail = ref[:, LB:]
        pick = lax.broadcasted_iota(jnp.int32, tail.shape, 1) == lane
        return jnp.sum(jnp.where(pick, tail, 0.0), axis=1, keepdims=True)

    pair = pl.program_id(0)
    lanes = PIECE + LB
    pieces = [(comp, i) for comp in range(2) for i in range(span // PIECE)]
    share = -(-len(pieces) // chunks)

    def build_piece(step, comp, i, dst):
        v0 = i * PIECE
        win = wpad_ref[step, comp:comp + 1, v0:v0 + lanes]
        tile = jnp.broadcast_to(win, (LB, lanes))
        rolled = pltpu.roll(tile, lanes - LB + 1, 1, stride=1, stride_axis=0)
        dst[comp * LB:(comp + 1) * LB, v0:v0 + PIECE] = rolled[:, :PIECE].astype(jnp.bfloat16)

    @pl.when(pair == 0)
    def _():
        acc[...] = jnp.zeros_like(acc)
        l_c = cos_ref[:, :LB]
        l_s = sin_ref[:, :LB]
        for i in range(CHUNK // LB):
            h_c = jnp.broadcast_to(column(cos_ref, groups + i), (LB, LB))
            h_s = jnp.broadcast_to(column(sin_ref, groups + i), (LB, LB))
            bc_ref[:, i * LB:(i + 1) * LB] = h_c * l_c - h_s * l_s
            bs_ref[:, i * LB:(i + 1) * LB] = h_s * l_c + h_c * l_s
        for comp, i in pieces:
            build_piece(0, comp, i, first_buf)

    offsets = [jnp.maximum(blocks_ref[q], 0) * LB for q in range(slots)]

    def one_step(step, cur, nxt, next_step):
        for c in range(chunks):
            g = step * chunks + c
            rr = ref_refs[0][g].astype(jnp.float32)
            for extra in ref_refs[1:]:
                rr = rr + extra[g].astype(jnp.float32)
            r_re = rr[0:1, :]
            r_im = rr[1:2, :]
            a_c = jnp.broadcast_to(column(cos_ref, g), (LB, CHUNK))
            a_s = jnp.broadcast_to(column(sin_ref, g), (LB, CHUNK))
            b_c = bc_ref[...]
            b_s = bs_ref[...]
            cos_part = a_c * b_c - a_s * b_s
            sine_part = a_s * b_c + a_c * b_s
            c_re = (r_re * cos_part - r_im * sine_part).astype(jnp.bfloat16)
            c_im = (0.0 - (r_re * sine_part + r_im * cos_part)).astype(jnp.bfloat16)
            coef = jnp.concatenate([c_re, c_im], axis=0)
            for q in range(slots):
                off = pl.multiple_of(offsets[q] + c * CHUNK, LB)
                hank = cur[:, pl.ds(off, CHUNK)]
                acc[q] += lax.dot_general(hank, coef, (((1,), (1,)), ((), ())),
                                          preferred_element_type=jnp.float32)
            for comp, i in pieces[c * share:(c + 1) * share]:
                build_piece(next_step, comp, i, nxt)

    step = 2 * pair
    one_step(step, first_buf, second_buf, step + 1)
    one_step(step + 1, second_buf, first_buf, jnp.minimum(step + 2, steps - 1))

    @pl.when(pair == pl.num_programs(0) - 1)
    def _():
        count = count_ref[0]
        for q in range(slots):
            part = acc[q]
            re = part[:LB, :LB] - part[LB:, LB:]
            im = part[:LB, LB:] + part[LB:, :LB]
            keep = q < count
            out_ref[q, 0] = jnp.where(keep, reverse_rows(re) * norm, 0.0)
            out_ref[q, 1] = jnp.where(keep, reverse_rows(im) * norm, 0.0)


def butterfly_sum(value, axes, later=(), rider=None):
    count = lax.axis_size(axes)
    stride = 1
    carried = None
    while stride < count:
        radix = 4 if stride * 4 <= count else 2
        parts = []
        for m in range(1, radix):
            pairs = [(i, i ^ (m * stride)) for i in range(count)]
            if stride == 1 and m == 1 and rider is not None:
                both = lax.ppermute(jnp.concatenate([value, rider], 0), axes, pairs)
                parts.append(both[:value.shape[0]])
                carried = both[value.shape[0]:]
            else:
                parts.append(lax.ppermute(value, axes, pairs))
        if stride * radix >= count:
            return [value] + parts, later, carried
        for part in parts:
            value = value + part
        if stride == 1:
            late = (value.reshape(-1)[0] != value.reshape(-1)[0]).astype(jnp.int32)
            later = jax.tree.map(lambda x: x + late.astype(x.dtype), later)
        stride *= radix
    return [value], later, carried


def seg_join(half, axis):
    count = lax.axis_size(axis)
    parts = lax.all_gather(half, axis, axis=half.ndim - 1, tiled=True) if count != 2 else None
    if parts is not None:
        return parts
    other = lax.ppermute(half, axis, [(0, 1), (1, 0)])
    first = lax.axis_index(axis) == 0
    return jnp.where(first, jnp.concatenate([half, other], -1), jnp.concatenate([other, half], -1))


def shards(surveillance, reference_blocks, owner_index, doppler_start, lag_blocks, block_count):
    segments = lax.axis_size("seg")
    seg_place = lax.axis_index("seg")
    beam_place = lax.axis_index("beam")
    seg_len = surveillance.shape[3]
    step_count = surveillance.shape[2]
    step_len = seg_len * segments
    window_len = step_count * step_len
    slot_count = lag_blocks.shape[1]
    rim_len = NLB * LB
    bins = DOP // segments
    chunks = step_len // CHUNK

    mine = (owner_index == beam_place)[None, :, None]
    local = jnp.where(mine, reference_blocks[0], jnp.zeros_like(reference_blocks[0]))
    group = lax.axis_size(("beam", "seg"))
    if segments == 2 and group >= 4 and not group & (group - 1) and seg_len == CHUNK:
        first = seg_place == 0
        own = jnp.transpose(local, (1, 0, 2))
        zero = jnp.zeros_like(own)
        placed = jnp.where(first, jnp.stack([own, zero], 1), jnp.stack([zero, own], 1)).reshape(-1, 2, seg_len)
        mine_samples = jnp.transpose(surveillance[0], (1, 0, 2))
        refparts, (first_bin,), other = butterfly_sum(placed, ("beam", "seg"), (doppler_start[0],), mine_samples)
        samples = jnp.where(first, jnp.concatenate([mine_samples, other], -1),
                            jnp.concatenate([other, mine_samples], -1))
    else:
        refs = seg_join(lax.psum(local, "beam"), "seg")
        refparts = [jnp.transpose(refs.reshape(2, step_count * chunks, CHUNK), (1, 0, 2))]
        samples = jnp.transpose(seg_join(surveillance[0], "seg"), (1, 0, 2))
        first_bin = doppler_start[0]

    span = step_len + rim_len
    wpad = samples.astype(jnp.float32)
    wpad = jnp.pad(wpad, ((0, 0), (0, 0), (0, span + LB - step_len)))

    freqs = first_bin + seg_place * bins + jnp.arange(bins, dtype=jnp.int32)
    times = jnp.concatenate([jnp.arange(LB, dtype=jnp.int32),
                             jnp.arange(step_count * chunks, dtype=jnp.int32) * CHUNK,
                             jnp.arange(CHUNK // LB, dtype=jnp.int32) * LB])
    cos_rows, sin_rows = phase_rows(freqs, times, window_len)
    tables = (cos_rows, sin_rows)
    assert step_count % 2 == 0
    kernel = functools.partial(caf_kernel, chunks=chunks, slots=slot_count, span=span, steps=step_count,
                               groups=step_count * chunks, parts=len(refparts),
                               norm=1.0 / math.sqrt(window_len))
    full = lambda shape: pl.BlockSpec(shape, lambda k, *_: (0,) * len(shape))
    out = pl.pallas_call(
        kernel,
        out_shape=jax.ShapeDtypeStruct((slot_count, 2, LB, bins), jnp.float32),
        grid_spec=pltpu.PrefetchScalarGridSpec(
            num_scalar_prefetch=2,
            grid=(step_count // 2,),
            in_specs=[full(wpad.shape)] + [full(t.shape) for t in tables] + [full(p.shape) for p in refparts],
            out_specs=full((slot_count, 2, LB, bins)),
            scratch_shapes=[pltpu.VMEM((2 * LB, span), jnp.bfloat16), pltpu.VMEM((2 * LB, span), jnp.bfloat16),
                            pltpu.VMEM((slot_count, 2 * LB, 2 * bins), jnp.float32),
                            pltpu.VMEM((bins, CHUNK), jnp.float32), pltpu.VMEM((bins, CHUNK), jnp.float32)],
        ),
        compiler_params=pltpu.CompilerParams(dimension_semantics=("arbitrary",)),
    )(lag_blocks[0], block_count, wpad, *tables, *refparts)
    return out[None]


def solution(mesh):
    placed = (
        P("beam", None, None, "seg"),
        P("beam", None, None, "seg"),
        P(),
        P("beam"),
        P("beam", None),
        P("beam"),
    )
    return jax.shard_map(
        shards,
        mesh=mesh,
        in_specs=placed,
        out_specs=P("beam", None, None, None, "seg"),
        check_vma=False,
    )
```

```python
import functools
import math

import jax
import jax.numpy as jnp
from jax import lax
from jax.experimental import pallas as pl
from jax.experimental.pallas import tpu as pltpu
from jax.sharding import PartitionSpec as P

LB = 128
NLB = 8
DOP = 256
CHUNK = 2048
PIECE = 1024


def phase_rows(freqs, times, window_len):
    turns = jnp.mod(freqs[:, None] * times[None, :], window_len)
    angle = turns.astype(jnp.float32) * (2.0 * math.pi / window_len)
    return jnp.cos(angle), jnp.sin(angle)


def reverse_rows(x):
    n = x.shape[0]
    rows = lax.broadcasted_iota(jnp.int32, (n, n), 0)
    cols = lax.broadcasted_iota(jnp.int32, (n, n), 1)
    flip = jnp.where(rows + cols == n - 1, 1.0, 0.0).astype(jnp.bfloat16)
    high = x.astype(jnp.bfloat16)
    rest = x - high.astype(jnp.float32)
    mid = rest.astype(jnp.bfloat16)
    low = (rest - mid.astype(jnp.float32)).astype(jnp.bfloat16)
    turn = lambda piece: jnp.dot(flip, piece, preferred_element_type=jnp.float32)
    return (turn(high) + turn(mid)) + turn(low)


def caf_kernel(blocks_ref, count_ref, wpad_ref, cos_ref, sin_ref, *rest, parts, chunks, slots, span, steps,
               groups, norm):
    ref_refs = rest[:parts]
    out_ref, first_buf, second_buf, acc, bc_ref, bs_ref = rest[parts:]
    def column(ref, lane):
        tail = ref[:, LB:]
        pick = lax.broadcasted_iota(jnp.int32, tail.shape, 1) == lane
        return jnp.sum(jnp.where(pick, tail, 0.0), axis=1, keepdims=True)

    pair = pl.program_id(0)
    lanes = PIECE + LB
    pieces = [(comp, i) for comp in range(2) for i in range(span // PIECE)]
    share = -(-len(pieces) // chunks)

    def build_piece(step, comp, i, dst):
        v0 = i * PIECE
        win = wpad_ref[step, comp:comp + 1, v0:v0 + lanes]
        tile = jnp.broadcast_to(win, (LB, lanes))
        rolled = pltpu.roll(tile, lanes - LB + 1, 1, stride=1, stride_axis=0)
        dst[comp * LB:(comp + 1) * LB, v0:v0 + PIECE] = rolled[:, :PIECE].astype(jnp.bfloat16)

    early = -(-(CHUNK + span - CHUNK * chunks - LB) // PIECE)
    head = [(comp, i) for comp, i in pieces if i < early]
    tail = [(comp, i) for comp, i in pieces if i >= early]

    @pl.when(pair == 0)
    def _():
        acc[...] = jnp.zeros_like(acc)
        l_c = cos_ref[:, :LB]
        l_s = sin_ref[:, :LB]
        for i in range(CHUNK // LB):
            h_c = jnp.broadcast_to(column(cos_ref, groups + i), (LB, LB))
            h_s = jnp.broadcast_to(column(sin_ref, groups + i), (LB, LB))
            bc_ref[:, i * LB:(i + 1) * LB] = h_c * l_c - h_s * l_s
            bs_ref[:, i * LB:(i + 1) * LB] = h_s * l_c + h_c * l_s
        for comp, i in head:
            build_piece(0, comp, i, first_buf)

    offsets = [jnp.maximum(blocks_ref[q], 0) * LB for q in range(slots)]

    def one_step(step, cur, nxt, next_step, fill=()):
        for c in range(chunks):
            g = step * chunks + c
            rr = ref_refs[0][g].astype(jnp.float32)
            for extra in ref_refs[1:]:
                rr = rr + extra[g].astype(jnp.float32)
            r_re = rr[0:1, :]
            r_im = rr[1:2, :]
            a_c = jnp.broadcast_to(column(cos_ref, g), (LB, CHUNK))
            a_s = jnp.broadcast_to(column(sin_ref, g), (LB, CHUNK))
            b_c = bc_ref[...]
            b_s = bs_ref[...]
            cos_part = a_c * b_c - a_s * b_s
            sine_part = a_s * b_c + a_c * b_s
            c_re = (r_re * cos_part - r_im * sine_part).astype(jnp.bfloat16)
            c_im = (0.0 - (r_re * sine_part + r_im * cos_part)).astype(jnp.bfloat16)
            coef = jnp.concatenate([c_re, c_im], axis=0)
            for q in range(slots):
                off = pl.multiple_of(offsets[q] + c * CHUNK, LB)
                hank = cur[:, pl.ds(off, CHUNK)]
                acc[q] += lax.dot_general(hank, coef, (((1,), (1,)), ((), ())),
                                          preferred_element_type=jnp.float32)
            if c == 0:
                for comp, i in fill:
                    build_piece(step, comp, i, cur)
            for comp, i in pieces[c * share:(c + 1) * share]:
                build_piece(next_step, comp, i, nxt)

    step = 2 * pair
    one_step(step, first_buf, second_buf, step + 1, tail)
    one_step(step + 1, second_buf, first_buf, jnp.minimum(step + 2, steps - 1))

    @pl.when(pair == pl.num_programs(0) - 1)
    def _():
        count = count_ref[0]
        for q in range(slots):
            part = acc[q]
            re = part[:LB, :LB] - part[LB:, LB:]
            im = part[:LB, LB:] + part[LB:, :LB]
            keep = q < count
            out_ref[q, 0] = jnp.where(keep, reverse_rows(re) * norm, 0.0)
            out_ref[q, 1] = jnp.where(keep, reverse_rows(im) * norm, 0.0)


def butterfly_sum(value, axes, later=(), rider=None):
    count = lax.axis_size(axes)
    stride = 1
    carried = None
    while stride < count:
        radix = 4 if stride * 4 <= count else 2
        parts = []
        for m in range(1, radix):
            pairs = [(i, i ^ (m * stride)) for i in range(count)]
            if stride == 1 and m == 1 and rider is not None:
                both = lax.ppermute(jnp.concatenate([value, rider], 0), axes, pairs)
                parts.append(both[:value.shape[0]])
                carried = both[value.shape[0]:]
            else:
                parts.append(lax.ppermute(value, axes, pairs))
        if stride * radix >= count:
            return [value] + parts, later, carried
        for part in parts:
            value = value + part
        if stride == 1:
            late = (value.reshape(-1)[0] != value.reshape(-1)[0]).astype(jnp.int32)
            later = jax.tree.map(lambda x: x + late.astype(x.dtype), later)
        stride *= radix
    return [value], later, carried


def seg_join(half, axis):
    count = lax.axis_size(axis)
    parts = lax.all_gather(half, axis, axis=half.ndim - 1, tiled=True) if count != 2 else None
    if parts is not None:
        return parts
    other = lax.ppermute(half, axis, [(0, 1), (1, 0)])
    first = lax.axis_index(axis) == 0
    return jnp.where(first, jnp.concatenate([half, other], -1), jnp.concatenate([other, half], -1))


def shards(surveillance, reference_blocks, owner_index, doppler_start, lag_blocks, block_count):
    segments = lax.axis_size("seg")
    seg_place = lax.axis_index("seg")
    beam_place = lax.axis_index("beam")
    seg_len = surveillance.shape[3]
    step_count = surveillance.shape[2]
    step_len = seg_len * segments
    window_len = step_count * step_len
    slot_count = lag_blocks.shape[1]
    rim_len = NLB * LB
    bins = DOP // segments
    chunks = step_len // CHUNK

    mine = (owner_index == beam_place)[None, :, None]
    local = jnp.where(mine, reference_blocks[0], jnp.zeros_like(reference_blocks[0]))
    group = lax.axis_size(("beam", "seg"))
    if segments == 2 and group >= 4 and not group & (group - 1) and seg_len == CHUNK:
        first = seg_place == 0
        own = jnp.transpose(local, (1, 0, 2))
        zero = jnp.zeros_like(own)
        placed = jnp.where(first, jnp.stack([own, zero], 1), jnp.stack([zero, own], 1)).reshape(-1, 2, seg_len)
        mine_samples = jnp.transpose(surveillance[0], (1, 0, 2))
        refparts, (first_bin,), other = butterfly_sum(placed, ("beam", "seg"), (doppler_start[0],), mine_samples)
        samples = jnp.where(first, jnp.concatenate([mine_samples, other], -1),
                            jnp.concatenate([other, mine_samples], -1))
    else:
        refs = seg_join(lax.psum(local, "beam"), "seg")
        refparts = [jnp.transpose(refs.reshape(2, step_count * chunks, CHUNK), (1, 0, 2))]
        samples = jnp.transpose(seg_join(surveillance[0], "seg"), (1, 0, 2))
        first_bin = doppler_start[0]

    span = step_len + rim_len
    wpad = samples.astype(jnp.float32)
    wpad = jnp.pad(wpad, ((0, 0), (0, 0), (0, span + LB - step_len)))

    freqs = first_bin + seg_place * bins + jnp.arange(bins, dtype=jnp.int32)
    times = jnp.concatenate([jnp.arange(LB, dtype=jnp.int32),
                             jnp.arange(step_count * chunks, dtype=jnp.int32) * CHUNK,
                             jnp.arange(CHUNK // LB, dtype=jnp.int32) * LB])
    cos_rows, sin_rows = phase_rows(freqs, times, window_len)
    tables = (cos_rows, sin_rows)
    assert step_count % 2 == 0
    kernel = functools.partial(caf_kernel, chunks=chunks, slots=slot_count, span=span, steps=step_count,
                               groups=step_count * chunks, parts=len(refparts),
                               norm=1.0 / math.sqrt(window_len))
    full = lambda shape: pl.BlockSpec(shape, lambda k, *_: (0,) * len(shape))
    out = pl.pallas_call(
        kernel,
        out_shape=jax.ShapeDtypeStruct((slot_count, 2, LB, bins), jnp.float32),
        grid_spec=pltpu.PrefetchScalarGridSpec(
            num_scalar_prefetch=2,
            grid=(step_count // 2,),
            in_specs=[full(wpad.shape)] + [full(t.shape) for t in tables] + [full(p.shape) for p in refparts],
            out_specs=full((slot_count, 2, LB, bins)),
            scratch_shapes=[pltpu.VMEM((2 * LB, span), jnp.bfloat16), pltpu.VMEM((2 * LB, span), jnp.bfloat16),
                            pltpu.VMEM((slot_count, 2 * LB, 2 * bins), jnp.float32),
                            pltpu.VMEM((bins, CHUNK), jnp.float32), pltpu.VMEM((bins, CHUNK), jnp.float32)],
        ),
        compiler_params=pltpu.CompilerParams(dimension_semantics=("arbitrary",)),
    )(lag_blocks[0], block_count, wpad, *tables, *refparts)
    return out[None]


def solution(mesh):
    placed = (
        P("beam", None, None, "seg"),
        P("beam", None, None, "seg"),
        P(),
        P("beam"),
        P("beam", None),
        P("beam"),
    )
    return jax.shard_map(
        shards,
        mesh=mesh,
        in_specs=placed,
        out_specs=P("beam", None, None, None, "seg"),
        check_vma=False,
    )
```

```python
import functools
import math

import jax
import jax.numpy as jnp
from jax import lax
from jax.experimental import pallas as pl
from jax.experimental.pallas import tpu as pltpu
from jax.sharding import PartitionSpec as P

LB = 128
NLB = 8
DOP = 256
CHUNK = 2048


def phase_rows(freqs, times, window_len):
    turns = jnp.mod(freqs[:, None] * times[None, :], window_len)
    angle = turns.astype(jnp.float32) * (2.0 * math.pi / window_len)
    return jnp.cos(angle), jnp.sin(angle)


def reverse_rows(x):
    n = x.shape[0]
    rows = lax.broadcasted_iota(jnp.int32, (n, n), 0)
    cols = lax.broadcasted_iota(jnp.int32, (n, n), 1)
    flip = jnp.where(rows + cols == n - 1, 1.0, 0.0).astype(jnp.bfloat16)
    high = x.astype(jnp.bfloat16)
    rest = x - high.astype(jnp.float32)
    mid = rest.astype(jnp.bfloat16)
    low = (rest - mid.astype(jnp.float32)).astype(jnp.bfloat16)
    turn = lambda piece: jnp.dot(flip, piece, preferred_element_type=jnp.float32)
    return (turn(high) + turn(mid)) + turn(low)


def caf_kernel(blocks_ref, count_ref, wpad_ref, cos_ref, sin_ref, *rest, parts, chunks, slots, span, steps,
               groups, norm):
    ref_refs = rest[:parts]
    out_ref, first_buf, second_buf, acc, bc_ref, bs_ref = rest[parts:]
    def column(ref, lane):
        tail = ref[:, LB:]
        pick = lax.broadcasted_iota(jnp.int32, tail.shape, 1) == lane
        return jnp.sum(jnp.where(pick, tail, 0.0), axis=1, keepdims=True)

    pair = pl.program_id(0)
    piece = span
    lanes = piece + LB
    pieces = [(comp, i) for comp in range(2) for i in range(span // piece)]
    share = -(-len(pieces) // chunks)

    def build_piece(step, comp, i, dst):
        v0 = i * piece
        win = wpad_ref[step, comp:comp + 1, v0:v0 + lanes]
        tile = jnp.broadcast_to(win, (LB, lanes))
        rolled = pltpu.roll(tile, lanes - LB + 1, 1, stride=1, stride_axis=0)
        dst[comp * LB:(comp + 1) * LB, v0:v0 + piece] = rolled[:, :piece].astype(jnp.bfloat16)

    @pl.when(pair == 0)
    def _():
        acc[...] = jnp.zeros_like(acc)
        l_c = cos_ref[:, :LB]
        l_s = sin_ref[:, :LB]
        for i in range(CHUNK // LB):
            h_c = jnp.broadcast_to(column(cos_ref, groups + i), (LB, LB))
            h_s = jnp.broadcast_to(column(sin_ref, groups + i), (LB, LB))
            bc_ref[:, i * LB:(i + 1) * LB] = h_c * l_c - h_s * l_s
            bs_ref[:, i * LB:(i + 1) * LB] = h_s * l_c + h_c * l_s
        for comp, i in pieces:
            build_piece(0, comp, i, first_buf)

    offsets = [jnp.maximum(blocks_ref[q], 0) * LB for q in range(slots)]

    def one_step(step, cur, nxt, next_step):
        for c in range(chunks):
            g = step * chunks + c
            rr = ref_refs[0][g].astype(jnp.float32)
            for extra in ref_refs[1:]:
                rr = rr + extra[g].astype(jnp.float32)
            r_re = rr[0:1, :]
            r_im = rr[1:2, :]
            a_c = jnp.broadcast_to(column(cos_ref, g), (LB, CHUNK))
            a_s = jnp.broadcast_to(column(sin_ref, g), (LB, CHUNK))
            b_c = bc_ref[...]
            b_s = bs_ref[...]
            cos_part = a_c * b_c - a_s * b_s
            sine_part = a_s * b_c + a_c * b_s
            c_re = (r_re * cos_part - r_im * sine_part).astype(jnp.bfloat16)
            c_im = (0.0 - (r_re * sine_part + r_im * cos_part)).astype(jnp.bfloat16)
            coef = jnp.concatenate([c_re, c_im], axis=0)
            for q in range(slots):
                off = pl.multiple_of(offsets[q] + c * CHUNK, LB)
                hank = cur[:, pl.ds(off, CHUNK)]
                acc[q] += lax.dot_general(hank, coef, (((1,), (1,)), ((), ())),
                                          preferred_element_type=jnp.float32)
            for comp, i in pieces[c * share:(c + 1) * share]:
                build_piece(next_step, comp, i, nxt)

    step = 2 * pair
    one_step(step, first_buf, second_buf, step + 1)
    one_step(step + 1, second_buf, first_buf, jnp.minimum(step + 2, steps - 1))

    @pl.when(pair == pl.num_programs(0) - 1)
    def _():
        count = count_ref[0]
        for q in range(slots):
            part = acc[q]
            re = part[:LB, :LB] - part[LB:, LB:]
            im = part[:LB, LB:] + part[LB:, :LB]
            keep = q < count
            out_ref[q, 0] = jnp.where(keep, reverse_rows(re) * norm, 0.0)
            out_ref[q, 1] = jnp.where(keep, reverse_rows(im) * norm, 0.0)


def butterfly_sum(value, axes, later=(), rider=None):
    count = lax.axis_size(axes)
    stride = 1
    carried = None
    while stride < count:
        radix = 4 if stride * 4 <= count else 2
        parts = []
        for m in range(1, radix):
            pairs = [(i, i ^ (m * stride)) for i in range(count)]
            if stride == 1 and m == 1 and rider is not None:
                both = lax.ppermute(jnp.concatenate([value, rider], 0), axes, pairs)
                parts.append(both[:value.shape[0]])
                carried = both[value.shape[0]:]
            else:
                parts.append(lax.ppermute(value, axes, pairs))
        if stride * radix >= count:
            return [value] + parts, later, carried
        for part in parts:
            value = value + part
        if stride == 1:
            late = (value.reshape(-1)[0] != value.reshape(-1)[0]).astype(jnp.int32)
            later = jax.tree.map(lambda x: x + late.astype(x.dtype), later)
        stride *= radix
    return [value], later, carried


def seg_join(half, axis):
    count = lax.axis_size(axis)
    parts = lax.all_gather(half, axis, axis=half.ndim - 1, tiled=True) if count != 2 else None
    if parts is not None:
        return parts
    other = lax.ppermute(half, axis, [(0, 1), (1, 0)])
    first = lax.axis_index(axis) == 0
    return jnp.where(first, jnp.concatenate([half, other], -1), jnp.concatenate([other, half], -1))


def shards(surveillance, reference_blocks, owner_index, doppler_start, lag_blocks, block_count):
    segments = lax.axis_size("seg")
    seg_place = lax.axis_index("seg")
    beam_place = lax.axis_index("beam")
    seg_len = surveillance.shape[3]
    step_count = surveillance.shape[2]
    step_len = seg_len * segments
    window_len = step_count * step_len
    slot_count = lag_blocks.shape[1]
    rim_len = NLB * LB
    bins = DOP // segments
    chunks = step_len // CHUNK

    mine = (owner_index == beam_place)[None, :, None]
    local = jnp.where(mine, reference_blocks[0], jnp.zeros_like(reference_blocks[0]))
    group = lax.axis_size(("beam", "seg"))
    if segments == 2 and group >= 4 and not group & (group - 1) and seg_len == CHUNK:
        first = seg_place == 0
        own = jnp.transpose(local, (1, 0, 2))
        zero = jnp.zeros_like(own)
        placed = jnp.where(first, jnp.stack([own, zero], 1), jnp.stack([zero, own], 1)).reshape(-1, 2, seg_len)
        mine_samples = jnp.transpose(surveillance[0], (1, 0, 2))
        refparts, (first_bin,), other = butterfly_sum(placed, ("beam", "seg"), (doppler_start[0],), mine_samples)
        samples = jnp.where(first, jnp.concatenate([mine_samples, other], -1),
                            jnp.concatenate([other, mine_samples], -1))
    else:
        refs = seg_join(lax.psum(local, "beam"), "seg")
        refparts = [jnp.transpose(refs.reshape(2, step_count * chunks, CHUNK), (1, 0, 2))]
        samples = jnp.transpose(seg_join(surveillance[0], "seg"), (1, 0, 2))
        first_bin = doppler_start[0]

    span = step_len + rim_len
    wpad = samples.astype(jnp.float32)
    wpad = jnp.pad(wpad, ((0, 0), (0, 0), (0, span + LB - step_len)))

    freqs = first_bin + seg_place * bins + jnp.arange(bins, dtype=jnp.int32)
    times = jnp.concatenate([jnp.arange(LB, dtype=jnp.int32),
                             jnp.arange(step_count * chunks, dtype=jnp.int32) * CHUNK,
                             jnp.arange(CHUNK // LB, dtype=jnp.int32) * LB])
    cos_rows, sin_rows = phase_rows(freqs, times, window_len)
    tables = (cos_rows, sin_rows)
    assert step_count % 2 == 0
    kernel = functools.partial(caf_kernel, chunks=chunks, slots=slot_count, span=span, steps=step_count,
                               groups=step_count * chunks, parts=len(refparts),
                               norm=1.0 / math.sqrt(window_len))
    full = lambda shape: pl.BlockSpec(shape, lambda k, *_: (0,) * len(shape))
    out = pl.pallas_call(
        kernel,
        out_shape=jax.ShapeDtypeStruct((slot_count, 2, LB, bins), jnp.float32),
        grid_spec=pltpu.PrefetchScalarGridSpec(
            num_scalar_prefetch=2,
            grid=(step_count // 2,),
            in_specs=[full(wpad.shape)] + [full(t.shape) for t in tables] + [full(p.shape) for p in refparts],
            out_specs=full((slot_count, 2, LB, bins)),
            scratch_shapes=[pltpu.VMEM((2 * LB, span), jnp.bfloat16), pltpu.VMEM((2 * LB, span), jnp.bfloat16),
                            pltpu.VMEM((slot_count, 2 * LB, 2 * bins), jnp.float32),
                            pltpu.VMEM((bins, CHUNK), jnp.float32), pltpu.VMEM((bins, CHUNK), jnp.float32)],
        ),
        compiler_params=pltpu.CompilerParams(dimension_semantics=("arbitrary",)),
    )(lag_blocks[0], block_count, wpad, *tables, *refparts)
    return out[None]


def solution(mesh):
    placed = (
        P("beam", None, None, "seg"),
        P("beam", None, None, "seg"),
        P(),
        P("beam"),
        P("beam", None),
        P("beam"),
    )
    return jax.shard_map(
        shards,
        mesh=mesh,
        in_specs=placed,
        out_specs=P("beam", None, None, None, "seg"),
        check_vma=False,
    )
```

```python
import functools
import math

import jax
import jax.numpy as jnp
from jax import lax
from jax.experimental import pallas as pl
from jax.experimental.pallas import tpu as pltpu
from jax.sharding import PartitionSpec as P

LB = 128
NLB = 8
DOP = 256
CHUNK = 4096


def phase_rows(freqs, times, window_len):
    turns = jnp.mod(freqs[:, None] * times[None, :], window_len)
    angle = turns.astype(jnp.float32) * (2.0 * math.pi / window_len)
    return jnp.cos(angle), jnp.sin(angle)


def reverse_rows(x):
    n = x.shape[0]
    rows = lax.broadcasted_iota(jnp.int32, (n, n), 0)
    cols = lax.broadcasted_iota(jnp.int32, (n, n), 1)
    flip = jnp.where(rows + cols == n - 1, 1.0, 0.0).astype(jnp.bfloat16)
    high = x.astype(jnp.bfloat16)
    rest = x - high.astype(jnp.float32)
    mid = rest.astype(jnp.bfloat16)
    low = (rest - mid.astype(jnp.float32)).astype(jnp.bfloat16)
    turn = lambda piece: jnp.dot(flip, piece, preferred_element_type=jnp.float32)
    return (turn(high) + turn(mid)) + turn(low)


def caf_kernel(blocks_ref, count_ref, wpad_ref, cos_ref, sin_ref, *rest, parts, chunks, slots, span, steps,
               groups, norm):
    ref_refs = rest[:parts]
    out_ref, first_buf, second_buf, acc, bc_ref, bs_ref = rest[parts:]
    def column(ref, lane):
        tail = ref[:, LB:]
        pick = lax.broadcasted_iota(jnp.int32, tail.shape, 1) == lane
        return jnp.sum(jnp.where(pick, tail, 0.0), axis=1, keepdims=True)

    pair = pl.program_id(0)
    piece = span
    lanes = piece + LB
    pieces = [(comp, i) for comp in range(2) for i in range(span // piece)]
    share = -(-len(pieces) // chunks)

    def build_piece(step, comp, i, dst):
        v0 = i * piece
        win = wpad_ref[step, comp:comp + 1, v0:v0 + lanes]
        tile = jnp.broadcast_to(win, (LB, lanes))
        rolled = pltpu.roll(tile, lanes - LB + 1, 1, stride=1, stride_axis=0)
        dst[comp * LB:(comp + 1) * LB, v0:v0 + piece] = rolled[:, :piece].astype(jnp.bfloat16)

    @pl.when(pair == 0)
    def _():
        acc[...] = jnp.zeros_like(acc)
        l_c = cos_ref[:, :LB]
        l_s = sin_ref[:, :LB]
        for i in range(CHUNK // LB):
            h_c = jnp.broadcast_to(column(cos_ref, groups + i), (LB, LB))
            h_s = jnp.broadcast_to(column(sin_ref, groups + i), (LB, LB))
            bc_ref[:, i * LB:(i + 1) * LB] = h_c * l_c - h_s * l_s
            bs_ref[:, i * LB:(i + 1) * LB] = h_s * l_c + h_c * l_s
        for comp, i in pieces:
            build_piece(0, comp, i, first_buf)

    offsets = [jnp.maximum(blocks_ref[q], 0) * LB for q in range(slots)]

    def one_step(step, cur, nxt, next_step):
        for c in range(chunks):
            g = step * chunks + c
            rr = ref_refs[0][g].astype(jnp.float32)
            for extra in ref_refs[1:]:
                rr = rr + extra[g].astype(jnp.float32)
            r_re = rr[0:1, :]
            r_im = rr[1:2, :]
            a_c = jnp.broadcast_to(column(cos_ref, g), (LB, CHUNK))
            a_s = jnp.broadcast_to(column(sin_ref, g), (LB, CHUNK))
            b_c = bc_ref[...]
            b_s = bs_ref[...]
            cos_part = a_c * b_c - a_s * b_s
            sine_part = a_s * b_c + a_c * b_s
            c_re = (r_re * cos_part - r_im * sine_part).astype(jnp.bfloat16)
            c_im = (0.0 - (r_re * sine_part + r_im * cos_part)).astype(jnp.bfloat16)
            coef = jnp.concatenate([c_re, c_im], axis=0)
            for q in range(slots):
                off = pl.multiple_of(offsets[q] + c * CHUNK, LB)
                hank = cur[:, pl.ds(off, CHUNK)]
                acc[q] += lax.dot_general(hank, coef, (((1,), (1,)), ((), ())),
                                          preferred_element_type=jnp.float32)
            for comp, i in pieces[c * share:(c + 1) * share]:
                build_piece(next_step, comp, i, nxt)

    step = 2 * pair
    one_step(step, first_buf, second_buf, step + 1)
    one_step(step + 1, second_buf, first_buf, jnp.minimum(step + 2, steps - 1))

    @pl.when(pair == pl.num_programs(0) - 1)
    def _():
        count = count_ref[0]
        for q in range(slots):
            part = acc[q]
            re = part[:LB, :LB] - part[LB:, LB:]
            im = part[:LB, LB:] + part[LB:, :LB]
            keep = q < count
            out_ref[q, 0] = jnp.where(keep, reverse_rows(re) * norm, 0.0)
            out_ref[q, 1] = jnp.where(keep, reverse_rows(im) * norm, 0.0)


def butterfly_sum(value, axes, later=(), rider=None):
    count = lax.axis_size(axes)
    stride = 1
    carried = None
    while stride < count:
        radix = 4 if stride * 4 <= count else 2
        parts = []
        for m in range(1, radix):
            pairs = [(i, i ^ (m * stride)) for i in range(count)]
            if stride == 1 and m == 1 and rider is not None:
                axis = -1 if value.shape[:-1] == rider.shape[:-1] else 0
                both = lax.ppermute(jnp.concatenate([value, rider], axis), axes, pairs)
                parts.append(lax.slice_in_dim(both, 0, value.shape[axis], axis=axis))
                carried = lax.slice_in_dim(both, value.shape[axis], both.shape[axis], axis=axis)
            else:
                parts.append(lax.ppermute(value, axes, pairs))
        if stride * radix >= count:
            return [value] + parts, later, carried
        for part in parts:
            value = value + part
        if stride == 1:
            late = (value.reshape(-1)[0] != value.reshape(-1)[0]).astype(jnp.int32)
            later = jax.tree.map(lambda x: x + late.astype(x.dtype), later)
        stride *= radix
    return [value], later, carried


def seg_join(half, axis):
    count = lax.axis_size(axis)
    parts = lax.all_gather(half, axis, axis=half.ndim - 1, tiled=True) if count != 2 else None
    if parts is not None:
        return parts
    other = lax.ppermute(half, axis, [(0, 1), (1, 0)])
    first = lax.axis_index(axis) == 0
    return jnp.where(first, jnp.concatenate([half, other], -1), jnp.concatenate([other, half], -1))


def shards(surveillance, reference_blocks, owner_index, doppler_start, lag_blocks, block_count):
    segments = lax.axis_size("seg")
    seg_place = lax.axis_index("seg")
    beam_place = lax.axis_index("beam")
    seg_len = surveillance.shape[3]
    step_count = surveillance.shape[2]
    step_len = seg_len * segments
    window_len = step_count * step_len
    slot_count = lag_blocks.shape[1]
    rim_len = NLB * LB
    bins = DOP // segments
    chunks = step_len // CHUNK

    mine = (owner_index == beam_place)[None, :, None]
    local = jnp.where(mine, reference_blocks[0], jnp.zeros_like(reference_blocks[0]))
    group = lax.axis_size(("beam", "seg"))
    if segments == 2 and group >= 4 and not group & (group - 1):
        first = seg_place == 0
        own = jnp.transpose(local, (1, 0, 2))
        zero = jnp.zeros_like(own)
        placed = jnp.where(first, jnp.concatenate([own, zero], -1), jnp.concatenate([zero, own], -1))
        placed = jnp.transpose(placed.reshape(step_count, 2, chunks, CHUNK), (0, 2, 1, 3)).reshape(-1, 2, CHUNK)
        mine_samples = jnp.transpose(surveillance[0], (1, 0, 2))
        refparts, (first_bin,), other = butterfly_sum(placed, ("beam", "seg"), (doppler_start[0],), mine_samples)
        samples = jnp.where(first, jnp.concatenate([mine_samples, other], -1),
                            jnp.concatenate([other, mine_samples], -1))
    else:
        refs = seg_join(lax.psum(local, "beam"), "seg")
        refparts = [jnp.transpose(refs.reshape(2, step_count * chunks, CHUNK), (1, 0, 2))]
        samples = jnp.transpose(seg_join(surveillance[0], "seg"), (1, 0, 2))
        first_bin = doppler_start[0]

    span = step_len + rim_len
    wpad = samples.astype(jnp.float32)
    wpad = jnp.pad(wpad, ((0, 0), (0, 0), (0, span + LB - step_len)))

    freqs = first_bin + seg_place * bins + jnp.arange(bins, dtype=jnp.int32)
    times = jnp.concatenate([jnp.arange(LB, dtype=jnp.int32),
                             jnp.arange(step_count * chunks, dtype=jnp.int32) * CHUNK,
                             jnp.arange(CHUNK // LB, dtype=jnp.int32) * LB])
    cos_rows, sin_rows = phase_rows(freqs, times, window_len)
    tables = (cos_rows, sin_rows)
    assert step_count % 2 == 0
    kernel = functools.partial(caf_kernel, chunks=chunks, slots=slot_count, span=span, steps=step_count,
                               groups=step_count * chunks, parts=len(refparts),
                               norm=1.0 / math.sqrt(window_len))
    full = lambda shape: pl.BlockSpec(shape, lambda k, *_: (0,) * len(shape))
    out = pl.pallas_call(
        kernel,
        out_shape=jax.ShapeDtypeStruct((slot_count, 2, LB, bins), jnp.float32),
        grid_spec=pltpu.PrefetchScalarGridSpec(
            num_scalar_prefetch=2,
            grid=(step_count // 2,),
            in_specs=[full(wpad.shape)] + [full(t.shape) for t in tables] + [full(p.shape) for p in refparts],
            out_specs=full((slot_count, 2, LB, bins)),
            scratch_shapes=[pltpu.VMEM((2 * LB, span), jnp.bfloat16), pltpu.VMEM((2 * LB, span), jnp.bfloat16),
                            pltpu.VMEM((slot_count, 2 * LB, 2 * bins), jnp.float32),
                            pltpu.VMEM((bins, CHUNK), jnp.float32), pltpu.VMEM((bins, CHUNK), jnp.float32)],
        ),
        compiler_params=pltpu.CompilerParams(dimension_semantics=("arbitrary",)),
    )(lag_blocks[0], block_count, wpad, *tables, *refparts)
    return out[None]


def solution(mesh):
    placed = (
        P("beam", None, None, "seg"),
        P("beam", None, None, "seg"),
        P(),
        P("beam"),
        P("beam", None),
        P("beam"),
    )
    return jax.shard_map(
        shards,
        mesh=mesh,
        in_specs=placed,
        out_specs=P("beam", None, None, None, "seg"),
        check_vma=False,
    )
```

```python
import functools
import math

import jax
import jax.numpy as jnp
from jax import lax
from jax.experimental import pallas as pl
from jax.experimental.pallas import tpu as pltpu
from jax.sharding import PartitionSpec as P

LB = 128
NLB = 8
DOP = 256
CHUNK = 2048
PIECE = 1024


def phase_rows(freqs, times, window_len):
    turns = jnp.mod(freqs[:, None] * times[None, :], window_len)
    angle = turns.astype(jnp.float32) * (2.0 * math.pi / window_len)
    return jnp.cos(angle), jnp.sin(angle)


def reverse_rows(x):
    n = x.shape[0]
    rows = lax.broadcasted_iota(jnp.int32, (n, n), 0)
    cols = lax.broadcasted_iota(jnp.int32, (n, n), 1)
    flip = jnp.where(rows + cols == n - 1, 1.0, 0.0).astype(jnp.bfloat16)
    high = x.astype(jnp.bfloat16)
    rest = x - high.astype(jnp.float32)
    mid = rest.astype(jnp.bfloat16)
    low = (rest - mid.astype(jnp.float32)).astype(jnp.bfloat16)
    turn = lambda piece: jnp.dot(flip, piece, preferred_element_type=jnp.float32)
    return (turn(high) + turn(mid)) + turn(low)


def caf_kernel(blocks_ref, count_ref, wpad_ref, cos_ref, sin_ref, *rest, parts, chunks, slots, span, steps,
               groups, norm):
    ref_refs = rest[:parts]
    out_ref, first_buf, second_buf, acc, bc_ref, bs_ref = rest[parts:]
    def column(ref, lane):
        tail = ref[:, LB:]
        pick = lax.broadcasted_iota(jnp.int32, tail.shape, 1) == lane
        return jnp.sum(jnp.where(pick, tail, 0.0), axis=1, keepdims=True)

    pair = pl.program_id(0)
    lanes = PIECE + LB
    pieces = [(comp, i) for comp in range(2) for i in range(span // PIECE)]
    share = -(-len(pieces) // chunks)

    def build_piece(step, comp, i, dst):
        v0 = i * PIECE
        win = wpad_ref[step, comp:comp + 1, v0:v0 + lanes]
        tile = jnp.broadcast_to(win, (LB, lanes))
        rolled = pltpu.roll(tile, lanes - LB + 1, 1, stride=1, stride_axis=0)
        dst[comp * LB:(comp + 1) * LB, v0:v0 + PIECE] = rolled[:, :PIECE].astype(jnp.bfloat16)

    @pl.when(pair == 0)
    def _():
        acc[...] = jnp.zeros_like(acc)
        l_c = cos_ref[:, :LB]
        l_s = sin_ref[:, :LB]
        for i in range(CHUNK // LB):
            h_c = jnp.broadcast_to(column(cos_ref, groups + i), (LB, LB))
            h_s = jnp.broadcast_to(column(sin_ref, groups + i), (LB, LB))
            bc_ref[:, i * LB:(i + 1) * LB] = h_c * l_c - h_s * l_s
            bs_ref[:, i * LB:(i + 1) * LB] = h_s * l_c + h_c * l_s
        for comp, i in pieces:
            build_piece(0, comp, i, first_buf)

    offsets = [jnp.maximum(blocks_ref[q], 0) * LB for q in range(slots)]

    def one_step(step, cur, nxt, next_step):
        for c in range(chunks):
            g = step * chunks + c
            rr = ref_refs[0][g].astype(jnp.float32)
            for extra in ref_refs[1:]:
                rr = rr + extra[g].astype(jnp.float32)
            r_re = rr[0:1, :]
            r_im = rr[1:2, :]
            a_c = jnp.broadcast_to(column(cos_ref, g), (LB, CHUNK))
            a_s = jnp.broadcast_to(column(sin_ref, g), (LB, CHUNK))
            b_c = bc_ref[...]
            b_s = bs_ref[...]
            cos_part = a_c * b_c - a_s * b_s
            sine_part = a_s * b_c + a_c * b_s
            c_re = (r_re * cos_part - r_im * sine_part).astype(jnp.bfloat16)
            c_im = (0.0 - (r_re * sine_part + r_im * cos_part)).astype(jnp.bfloat16)
            coef = jnp.concatenate([c_re, c_im], axis=0)
            for q in range(slots):
                off = pl.multiple_of(offsets[q] + c * CHUNK, LB)
                hank = cur[:, pl.ds(off, CHUNK)]
                acc[q] += lax.dot_general(hank, coef, (((1,), (1,)), ((), ())),
                                          preferred_element_type=jnp.float32)
            for comp, i in pieces[c * share:(c + 1) * share]:
                build_piece(next_step, comp, i, nxt)

    step = 2 * pair
    one_step(step, first_buf, second_buf, step + 1)
    one_step(step + 1, second_buf, first_buf, jnp.minimum(step + 2, steps - 1))

    @pl.when(pair == pl.num_programs(0) - 1)
    def _():
        count = count_ref[0]
        for q in range(slots):
            part = acc[q]
            re = part[:LB, :LB] - part[LB:, LB:]
            im = part[:LB, LB:] + part[LB:, :LB]
            keep = q < count
            out_ref[q, 0] = jnp.where(keep, reverse_rows(re) * norm, 0.0)
            out_ref[q, 1] = jnp.where(keep, reverse_rows(im) * norm, 0.0)


def butterfly_sum(value, axes, later=(), rider=None):
    count = lax.axis_size(axes)
    stride = 1
    carried = None
    while stride < count:
        radix = 4 if stride * 4 <= count else 2
        parts = []
        for m in range(1, radix):
            pairs = [(i, i ^ (m * stride)) for i in range(count)]
            if stride == 1 and m == 1 and rider is not None:
                both = lax.ppermute(jnp.concatenate([value, rider], 0), axes, pairs)
                parts.append(both[:value.shape[0]])
                carried = both[value.shape[0]:]
            else:
                parts.append(lax.ppermute(value, axes, pairs))
        if stride * radix >= count:
            return [value] + parts, later, carried
        for part in parts:
            value = value + part
        if stride == 1:
            late = (value.reshape(-1)[0] != value.reshape(-1)[0]).astype(jnp.int32)
            later = jax.tree.map(lambda x: x + late.astype(x.dtype), later)
        stride *= radix
    return [value], later, carried


def seg_join(half, axis):
    count = lax.axis_size(axis)
    parts = lax.all_gather(half, axis, axis=half.ndim - 1, tiled=True) if count != 2 else None
    if parts is not None:
        return parts
    other = lax.ppermute(half, axis, [(0, 1), (1, 0)])
    first = lax.axis_index(axis) == 0
    return jnp.where(first, jnp.concatenate([half, other], -1), jnp.concatenate([other, half], -1))


def shards(surveillance, reference_blocks, owner_index, doppler_start, lag_blocks, block_count):
    segments = lax.axis_size("seg")
    seg_place = lax.axis_index("seg")
    beam_place = lax.axis_index("beam")
    seg_len = surveillance.shape[3]
    step_count = surveillance.shape[2]
    step_len = seg_len * segments
    window_len = step_count * step_len
    slot_count = lag_blocks.shape[1]
    rim_len = NLB * LB
    bins = DOP // segments
    chunks = step_len // CHUNK

    mine = jnp.stack([owner_index[k] == beam_place for k in range(step_count)])[None, :, None]
    local = jnp.where(mine, reference_blocks[0], jnp.zeros_like(reference_blocks[0]))
    group = lax.axis_size(("beam", "seg"))
    if segments == 2 and group >= 4 and not group & (group - 1) and seg_len == CHUNK:
        first = seg_place == 0
        own = jnp.transpose(local, (1, 0, 2))
        zero = jnp.zeros_like(own)
        placed = jnp.where(first, jnp.stack([own, zero], 1), jnp.stack([zero, own], 1)).reshape(-1, 2, seg_len)
        mine_samples = jnp.transpose(surveillance[0], (1, 0, 2))
        refparts, (first_bin,), other = butterfly_sum(placed, ("beam", "seg"), (doppler_start[0],), mine_samples)
        samples = jnp.where(first, jnp.concatenate([mine_samples, other], -1),
                            jnp.concatenate([other, mine_samples], -1))
    else:
        refs = seg_join(lax.psum(local, "beam"), "seg")
        refparts = [jnp.transpose(refs.reshape(2, step_count * chunks, CHUNK), (1, 0, 2))]
        samples = jnp.transpose(seg_join(surveillance[0], "seg"), (1, 0, 2))
        first_bin = doppler_start[0]

    span = step_len + rim_len
    wpad = samples.astype(jnp.float32)
    wpad = jnp.pad(wpad, ((0, 0), (0, 0), (0, span + LB - step_len)))

    freqs = first_bin + seg_place * bins + jnp.arange(bins, dtype=jnp.int32)
    times = jnp.concatenate([jnp.arange(LB, dtype=jnp.int32),
                             jnp.arange(step_count * chunks, dtype=jnp.int32) * CHUNK,
                             jnp.arange(CHUNK // LB, dtype=jnp.int32) * LB])
    cos_rows, sin_rows = phase_rows(freqs, times, window_len)
    tables = (cos_rows, sin_rows)
    assert step_count % 2 == 0
    kernel = functools.partial(caf_kernel, chunks=chunks, slots=slot_count, span=span, steps=step_count,
                               groups=step_count * chunks, parts=len(refparts),
                               norm=1.0 / math.sqrt(window_len))
    full = lambda shape: pl.BlockSpec(shape, lambda k, *_: (0,) * len(shape))
    out = pl.pallas_call(
        kernel,
        out_shape=jax.ShapeDtypeStruct((slot_count, 2, LB, bins), jnp.float32),
        grid_spec=pltpu.PrefetchScalarGridSpec(
            num_scalar_prefetch=2,
            grid=(step_count // 2,),
            in_specs=[full(wpad.shape)] + [full(t.shape) for t in tables] + [full(p.shape) for p in refparts],
            out_specs=full((slot_count, 2, LB, bins)),
            scratch_shapes=[pltpu.VMEM((2 * LB, span), jnp.bfloat16), pltpu.VMEM((2 * LB, span), jnp.bfloat16),
                            pltpu.VMEM((slot_count, 2 * LB, 2 * bins), jnp.float32),
                            pltpu.VMEM((bins, CHUNK), jnp.float32), pltpu.VMEM((bins, CHUNK), jnp.float32)],
        ),
        compiler_params=pltpu.CompilerParams(dimension_semantics=("arbitrary",)),
    )(lag_blocks[0], block_count, wpad, *tables, *refparts)
    return out[None]


def solution(mesh):
    placed = (
        P("beam", None, None, "seg"),
        P("beam", None, None, "seg"),
        P(),
        P("beam"),
        P("beam", None),
        P("beam"),
    )
    return jax.shard_map(
        shards,
        mesh=mesh,
        in_specs=placed,
        out_specs=P("beam", None, None, None, "seg"),
        check_vma=False,
    )
```

```python
import functools
import math

import jax
import jax.numpy as jnp
from jax import lax
from jax.experimental import pallas as pl
from jax.experimental.pallas import tpu as pltpu
from jax.sharding import PartitionSpec as P

LB = 128
NLB = 8
DOP = 256
CHUNK = 2048
PIECE = 1024


def phase_rows(freqs, times, window_len):
    turns = jnp.mod(freqs[:, None] * times[None, :], window_len)
    angle = turns.astype(jnp.float32) * (2.0 * math.pi / window_len)
    return jnp.cos(angle), jnp.sin(angle)


def reverse_rows(x):
    n = x.shape[0]
    rows = lax.broadcasted_iota(jnp.int32, (n, n), 0)
    cols = lax.broadcasted_iota(jnp.int32, (n, n), 1)
    flip = jnp.where(rows + cols == n - 1, 1.0, 0.0).astype(jnp.bfloat16)
    high = x.astype(jnp.bfloat16)
    rest = x - high.astype(jnp.float32)
    mid = rest.astype(jnp.bfloat16)
    low = (rest - mid.astype(jnp.float32)).astype(jnp.bfloat16)
    turn = lambda piece: jnp.dot(flip, piece, preferred_element_type=jnp.float32)
    return (turn(high) + turn(mid)) + turn(low)


def caf_kernel(blocks_ref, count_ref, wpad_ref, cos_ref, sin_ref, *rest, parts, chunks, slots, span, steps,
               groups, norm):
    ref_refs = rest[:parts]
    out_ref, first_buf, second_buf, acc, bc_ref, bs_ref = rest[parts:]
    def column(ref, lane):
        tail = ref[:, LB:]
        pick = lax.broadcasted_iota(jnp.int32, tail.shape, 1) == lane
        return jnp.sum(jnp.where(pick, tail, 0.0), axis=1, keepdims=True)

    pair = pl.program_id(0)
    lanes = PIECE + LB
    pieces = [(comp, i) for comp in range(2) for i in range(span // PIECE)]
    share = -(-len(pieces) // chunks)

    def build_piece(step, comp, i, dst):
        v0 = i * PIECE
        win = wpad_ref[step, comp:comp + 1, v0:v0 + lanes]
        tile = jnp.broadcast_to(win, (LB, lanes))
        rolled = pltpu.roll(tile, lanes - LB + 1, 1, stride=1, stride_axis=0)
        dst[comp * LB:(comp + 1) * LB, v0:v0 + PIECE] = rolled[:, :PIECE].astype(jnp.bfloat16)

    @pl.when(pair == 0)
    def _():
        acc[...] = jnp.zeros_like(acc)
        l_c = cos_ref[:, :LB]
        l_s = sin_ref[:, :LB]
        for i in range(CHUNK // LB):
            h_c = jnp.broadcast_to(column(cos_ref, groups + i), (LB, LB))
            h_s = jnp.broadcast_to(column(sin_ref, groups + i), (LB, LB))
            bc_ref[:, i * LB:(i + 1) * LB] = h_c * l_c - h_s * l_s
            bs_ref[:, i * LB:(i + 1) * LB] = h_s * l_c + h_c * l_s
        for comp, i in pieces:
            build_piece(0, comp, i, first_buf)

    offsets = [jnp.maximum(blocks_ref[q], 0) * LB for q in range(slots)]

    def one_step(step, cur, nxt, next_step):
        for c in range(chunks):
            g = step * chunks + c
            rr = ref_refs[0][g].astype(jnp.float32)
            for extra in ref_refs[1:]:
                rr = rr + extra[g].astype(jnp.float32)
            r_re = rr[0:1, :]
            r_im = rr[1:2, :]
            a_c = jnp.broadcast_to(column(cos_ref, g), (LB, CHUNK))
            a_s = jnp.broadcast_to(column(sin_ref, g), (LB, CHUNK))
            b_c = bc_ref[...]
            b_s = bs_ref[...]
            cos_part = a_c * b_c - a_s * b_s
            sine_part = a_s * b_c + a_c * b_s
            c_re = (r_re * cos_part - r_im * sine_part).astype(jnp.bfloat16)
            c_im = (0.0 - (r_re * sine_part + r_im * cos_part)).astype(jnp.bfloat16)
            coef = jnp.concatenate([c_re, c_im], axis=0)
            for q in range(slots):
                off = pl.multiple_of(offsets[q] + c * CHUNK, LB)
                hank = cur[:, pl.ds(off, CHUNK)]
                acc[q] += lax.dot_general(hank, coef, (((1,), (1,)), ((), ())),
                                          preferred_element_type=jnp.float32)
            for comp, i in pieces[c * share:(c + 1) * share]:
                build_piece(next_step, comp, i, nxt)

    step = 2 * pair
    one_step(step, first_buf, second_buf, step + 1)
    one_step(step + 1, second_buf, first_buf, jnp.minimum(step + 2, steps - 1))

    @pl.when(pair == pl.num_programs(0) - 1)
    def _():
        count = count_ref[0]
        for q in range(slots):
            part = acc[q]
            re = part[:LB, :LB] - part[LB:, LB:]
            im = part[:LB, LB:] + part[LB:, :LB]
            keep = q < count
            out_ref[q, 0] = jnp.where(keep, reverse_rows(re) * norm, 0.0)
            out_ref[q, 1] = jnp.where(keep, reverse_rows(im) * norm, 0.0)


def butterfly_sum(value, axes, later=(), rider=None, stride=1):
    count = lax.axis_size(axes)
    carried = None
    while stride < count:
        radix = 4 if stride * 4 <= count else 2
        parts = []
        for m in range(1, radix):
            pairs = [(i, i ^ (m * stride)) for i in range(count)]
            if stride == 1 and m == 1 and rider is not None:
                both = lax.ppermute(jnp.concatenate([value, rider], 0), axes, pairs)
                parts.append(both[:value.shape[0]])
                carried = both[value.shape[0]:]
            else:
                parts.append(lax.ppermute(value, axes, pairs))
        if stride * radix >= count:
            return [value] + parts, later, carried
        for part in parts:
            value = value + part
        if stride == 1:
            late = (value.reshape(-1)[0] != value.reshape(-1)[0]).astype(jnp.int32)
            later = jax.tree.map(lambda x: x + late.astype(x.dtype), later)
        stride *= radix
    return [value], later, carried


def seg_join(half, axis):
    count = lax.axis_size(axis)
    parts = lax.all_gather(half, axis, axis=half.ndim - 1, tiled=True) if count != 2 else None
    if parts is not None:
        return parts
    other = lax.ppermute(half, axis, [(0, 1), (1, 0)])
    first = lax.axis_index(axis) == 0
    return jnp.where(first, jnp.concatenate([half, other], -1), jnp.concatenate([other, half], -1))


def shards(surveillance, reference_blocks, owner_index, doppler_start, lag_blocks, block_count):
    segments = lax.axis_size("seg")
    seg_place = lax.axis_index("seg")
    beam_place = lax.axis_index("beam")
    seg_len = surveillance.shape[3]
    step_count = surveillance.shape[2]
    step_len = seg_len * segments
    window_len = step_count * step_len
    slot_count = lag_blocks.shape[1]
    rim_len = NLB * LB
    bins = DOP // segments
    chunks = step_len // CHUNK

    mine = (owner_index == beam_place)[None, :, None]
    local = jnp.where(mine, reference_blocks[0], jnp.zeros_like(reference_blocks[0]))
    group = lax.axis_size(("beam", "seg"))
    if segments == 2 and group >= 16 and not group & (group - 1) and seg_len == CHUNK:
        axes = ("beam", "seg")
        first = seg_place == 0
        own = jnp.transpose(local, (1, 0, 2))
        mine_samples = jnp.transpose(surveillance[0], (1, 0, 2))
        swap = lambda x, m: lax.ppermute(x, axes, [(i, i ^ m) for i in range(group)])
        partner = swap(jnp.concatenate([own, mine_samples], 0), 1)
        same_half = own + swap(own, 2)
        other_half = partner[:step_count] + swap(own, 3)
        other = partner[step_count:]
        placed = jnp.where(first, jnp.stack([same_half, other_half], 1),
                           jnp.stack([other_half, same_half], 1)).reshape(-1, 2, seg_len)
        late = (placed.reshape(-1)[0] != placed.reshape(-1)[0]).astype(jnp.int32)
        first_bin = doppler_start[0] + late
        refparts, _, _ = butterfly_sum(placed, axes, stride=4)
        samples = jnp.where(first, jnp.concatenate([mine_samples, other], -1),
                            jnp.concatenate([other, mine_samples], -1))
    else:
        refs = seg_join(lax.psum(local, "beam"), "seg")
        refparts = [jnp.transpose(refs.reshape(2, step_count * chunks, CHUNK), (1, 0, 2))]
        samples = jnp.transpose(seg_join(surveillance[0], "seg"), (1, 0, 2))
        first_bin = doppler_start[0]

    span = step_len + rim_len
    wpad = samples.astype(jnp.float32)
    wpad = jnp.pad(wpad, ((0, 0), (0, 0), (0, span + LB - step_len)))

    freqs = first_bin + seg_place * bins + jnp.arange(bins, dtype=jnp.int32)
    times = jnp.concatenate([jnp.arange(LB, dtype=jnp.int32),
                             jnp.arange(step_count * chunks, dtype=jnp.int32) * CHUNK,
                             jnp.arange(CHUNK // LB, dtype=jnp.int32) * LB])
    cos_rows, sin_rows = phase_rows(freqs, times, window_len)
    tables = (cos_rows, sin_rows)
    assert step_count % 2 == 0
    kernel = functools.partial(caf_kernel, chunks=chunks, slots=slot_count, span=span, steps=step_count,
                               groups=step_count * chunks, parts=len(refparts),
                               norm=1.0 / math.sqrt(window_len))
    full = lambda shape: pl.BlockSpec(shape, lambda k, *_: (0,) * len(shape))
    out = pl.pallas_call(
        kernel,
        out_shape=jax.ShapeDtypeStruct((slot_count, 2, LB, bins), jnp.float32),
        grid_spec=pltpu.PrefetchScalarGridSpec(
            num_scalar_prefetch=2,
            grid=(step_count // 2,),
            in_specs=[full(wpad.shape)] + [full(t.shape) for t in tables] + [full(p.shape) for p in refparts],
            out_specs=full((slot_count, 2, LB, bins)),
            scratch_shapes=[pltpu.VMEM((2 * LB, span), jnp.bfloat16), pltpu.VMEM((2 * LB, span), jnp.bfloat16),
                            pltpu.VMEM((slot_count, 2 * LB, 2 * bins), jnp.float32),
                            pltpu.VMEM((bins, CHUNK), jnp.float32), pltpu.VMEM((bins, CHUNK), jnp.float32)],
        ),
        compiler_params=pltpu.CompilerParams(dimension_semantics=("arbitrary",)),
    )(lag_blocks[0], block_count, wpad, *tables, *refparts)
    return out[None]


def solution(mesh):
    placed = (
        P("beam", None, None, "seg"),
        P("beam", None, None, "seg"),
        P(),
        P("beam"),
        P("beam", None),
        P("beam"),
    )
    return jax.shard_map(
        shards,
        mesh=mesh,
        in_specs=placed,
        out_specs=P("beam", None, None, None, "seg"),
        check_vma=False,
    )
```

```python
import functools
import math

import jax
import jax.numpy as jnp
from jax import lax
from jax.experimental import pallas as pl
from jax.experimental.pallas import tpu as pltpu
from jax.sharding import PartitionSpec as P

LB = 128
NLB = 8
DOP = 256
CHUNK = 2048


def phase_rows(freqs, times, window_len):
    turns = jnp.mod(freqs[:, None] * times[None, :], window_len)
    angle = turns.astype(jnp.float32) * (2.0 * math.pi / window_len)
    return jnp.cos(angle), jnp.sin(angle)


def reverse_rows(x):
    n = x.shape[0]
    rows = lax.broadcasted_iota(jnp.int32, (n, n), 0)
    cols = lax.broadcasted_iota(jnp.int32, (n, n), 1)
    flip = jnp.where(rows + cols == n - 1, 1.0, 0.0).astype(jnp.bfloat16)
    high = x.astype(jnp.bfloat16)
    rest = x - high.astype(jnp.float32)
    mid = rest.astype(jnp.bfloat16)
    low = (rest - mid.astype(jnp.float32)).astype(jnp.bfloat16)
    turn = lambda piece: jnp.dot(flip, piece, preferred_element_type=jnp.float32)
    return (turn(high) + turn(mid)) + turn(low)


def caf_kernel(blocks_ref, count_ref, wpad_ref, cos_ref, sin_ref, *rest, parts, chunks, slots, span, steps,
               groups, norm):
    ref_refs = rest[:parts]
    out_ref, first_buf, second_buf, acc, bc_ref, bs_ref = rest[parts:]
    def column(ref, lane):
        tail = ref[:, LB:]
        pick = lax.broadcasted_iota(jnp.int32, tail.shape, 1) == lane
        return jnp.sum(jnp.where(pick, tail, 0.0), axis=1, keepdims=True)

    pair = pl.program_id(0)
    piece = span
    lanes = piece + LB
    pieces = [(comp, i) for comp in range(2) for i in range(span // piece)]
    share = -(-len(pieces) // chunks)

    def build_piece(step, comp, i, dst):
        v0 = i * piece
        win = wpad_ref[step, comp:comp + 1, v0:v0 + lanes]
        tile = jnp.broadcast_to(win, (LB, lanes))
        rolled = pltpu.roll(tile, lanes - LB + 1, 1, stride=1, stride_axis=0)
        dst[comp * LB:(comp + 1) * LB, v0:v0 + piece] = rolled[:, :piece].astype(jnp.bfloat16)

    @pl.when(pair == 0)
    def _():
        acc[...] = jnp.zeros_like(acc)
        l_c = cos_ref[:, :LB]
        l_s = sin_ref[:, :LB]
        for i in range(CHUNK // LB):
            h_c = jnp.broadcast_to(column(cos_ref, groups + i), (LB, LB))
            h_s = jnp.broadcast_to(column(sin_ref, groups + i), (LB, LB))
            bc_ref[:, i * LB:(i + 1) * LB] = h_c * l_c - h_s * l_s
            bs_ref[:, i * LB:(i + 1) * LB] = h_s * l_c + h_c * l_s
        for comp, i in pieces:
            build_piece(0, comp, i, first_buf)

    offsets = [jnp.maximum(blocks_ref[q], 0) * LB for q in range(slots)]

    def one_step(step, cur, nxt, next_step):
        for c in range(chunks):
            g = step * chunks + c
            rr = ref_refs[0][g].astype(jnp.float32)
            for extra in ref_refs[1:]:
                rr = rr + extra[g].astype(jnp.float32)
            r_re = rr[0:1, :]
            r_im = rr[1:2, :]
            a_c = jnp.broadcast_to(column(cos_ref, g), (LB, CHUNK))
            a_s = jnp.broadcast_to(column(sin_ref, g), (LB, CHUNK))
            b_c = bc_ref[...]
            b_s = bs_ref[...]
            cos_part = a_c * b_c - a_s * b_s
            sine_part = a_s * b_c + a_c * b_s
            c_re = (r_re * cos_part - r_im * sine_part).astype(jnp.bfloat16)
            c_im = (0.0 - (r_re * sine_part + r_im * cos_part)).astype(jnp.bfloat16)
            coef = jnp.concatenate([c_re, c_im], axis=0)
            for q in range(slots):
                off = pl.multiple_of(offsets[q] + c * CHUNK, LB)
                hank = cur[:, pl.ds(off, CHUNK)]
                acc[q] += lax.dot_general(hank, coef, (((1,), (1,)), ((), ())),
                                          preferred_element_type=jnp.float32)
            for comp, i in pieces[c * share:(c + 1) * share]:
                build_piece(next_step, comp, i, nxt)

    step = 2 * pair
    one_step(step, first_buf, second_buf, step + 1)
    one_step(step + 1, second_buf, first_buf, jnp.minimum(step + 2, steps - 1))

    @pl.when(pair == pl.num_programs(0) - 1)
    def _():
        count = count_ref[0]
        for q in range(slots):
            part = acc[q]
            re = part[:LB, :LB] - part[LB:, LB:]
            im = part[:LB, LB:] + part[LB:, :LB]
            keep = q < count
            out_ref[q, 0] = jnp.where(keep, reverse_rows(re) * norm, 0.0)
            out_ref[q, 1] = jnp.where(keep, reverse_rows(im) * norm, 0.0)


def butterfly_sum(value, axes, later=(), rider=None, stride=1):
    count = lax.axis_size(axes)
    carried = None
    while stride < count:
        radix = 4 if stride * 4 <= count else 2
        parts = []
        for m in range(1, radix):
            pairs = [(i, i ^ (m * stride)) for i in range(count)]
            if stride == 1 and m == 1 and rider is not None:
                both = lax.ppermute(jnp.concatenate([value, rider], 0), axes, pairs)
                parts.append(both[:value.shape[0]])
                carried = both[value.shape[0]:]
            else:
                parts.append(lax.ppermute(value, axes, pairs))
        if stride * radix >= count:
            return [value] + parts, later, carried
        for part in parts:
            value = value + part
        if stride == 1:
            late = (value.reshape(-1)[0] != value.reshape(-1)[0]).astype(jnp.int32)
            later = jax.tree.map(lambda x: x + late.astype(x.dtype), later)
        stride *= radix
    return [value], later, carried


def seg_join(half, axis):
    count = lax.axis_size(axis)
    parts = lax.all_gather(half, axis, axis=half.ndim - 1, tiled=True) if count != 2 else None
    if parts is not None:
        return parts
    other = lax.ppermute(half, axis, [(0, 1), (1, 0)])
    first = lax.axis_index(axis) == 0
    return jnp.where(first, jnp.concatenate([half, other], -1), jnp.concatenate([other, half], -1))


def shards(surveillance, reference_blocks, owner_index, doppler_start, lag_blocks, block_count):
    segments = lax.axis_size("seg")
    seg_place = lax.axis_index("seg")
    beam_place = lax.axis_index("beam")
    seg_len = surveillance.shape[3]
    step_count = surveillance.shape[2]
    step_len = seg_len * segments
    window_len = step_count * step_len
    slot_count = lag_blocks.shape[1]
    rim_len = NLB * LB
    bins = DOP // segments
    chunks = step_len // CHUNK

    mine = (owner_index == beam_place)[None, :, None]
    local = jnp.where(mine, reference_blocks[0], jnp.zeros_like(reference_blocks[0]))
    group = lax.axis_size(("beam", "seg"))
    if segments == 2 and group >= 16 and not group & (group - 1) and seg_len == CHUNK:
        axes = ("beam", "seg")
        first = seg_place == 0
        own = jnp.transpose(local, (1, 0, 2))
        mine_samples = jnp.transpose(surveillance[0], (1, 0, 2))
        swap = lambda x, m: lax.ppermute(x, axes, [(i, i ^ m) for i in range(group)])
        partner = swap(jnp.concatenate([own, mine_samples], 0), 1)
        same_half = own + swap(own, 2)
        other_half = partner[:step_count] + swap(own, 3)
        other = partner[step_count:]
        placed = jnp.where(first, jnp.stack([same_half, other_half], 1),
                           jnp.stack([other_half, same_half], 1)).reshape(-1, 2, seg_len)
        late = (placed.reshape(-1)[0] != placed.reshape(-1)[0]).astype(jnp.int32)
        first_bin = doppler_start[0] + late
        refparts, _, _ = butterfly_sum(placed, axes, stride=4)
        samples = jnp.where(first, jnp.concatenate([mine_samples, other], -1),
                            jnp.concatenate([other, mine_samples], -1))
    else:
        refs = seg_join(lax.psum(local, "beam"), "seg")
        refparts = [jnp.transpose(refs.reshape(2, step_count * chunks, CHUNK), (1, 0, 2))]
        samples = jnp.transpose(seg_join(surveillance[0], "seg"), (1, 0, 2))
        first_bin = doppler_start[0]

    span = step_len + rim_len
    wpad = samples.astype(jnp.float32)
    wpad = jnp.pad(wpad, ((0, 0), (0, 0), (0, span + LB - step_len)))

    freqs = first_bin + seg_place * bins + jnp.arange(bins, dtype=jnp.int32)
    times = jnp.concatenate([jnp.arange(LB, dtype=jnp.int32),
                             jnp.arange(step_count * chunks, dtype=jnp.int32) * CHUNK,
                             jnp.arange(CHUNK // LB, dtype=jnp.int32) * LB])
    cos_rows, sin_rows = phase_rows(freqs, times, window_len)
    tables = (cos_rows, sin_rows)
    assert step_count % 2 == 0
    kernel = functools.partial(caf_kernel, chunks=chunks, slots=slot_count, span=span, steps=step_count,
                               groups=step_count * chunks, parts=len(refparts),
                               norm=1.0 / math.sqrt(window_len))
    full = lambda shape: pl.BlockSpec(shape, lambda k, *_: (0,) * len(shape))
    out = pl.pallas_call(
        kernel,
        out_shape=jax.ShapeDtypeStruct((slot_count, 2, LB, bins), jnp.float32),
        grid_spec=pltpu.PrefetchScalarGridSpec(
            num_scalar_prefetch=2,
            grid=(step_count // 2,),
            in_specs=[full(wpad.shape)] + [full(t.shape) for t in tables] + [full(p.shape) for p in refparts],
            out_specs=full((slot_count, 2, LB, bins)),
            scratch_shapes=[pltpu.VMEM((2 * LB, span), jnp.bfloat16), pltpu.VMEM((2 * LB, span), jnp.bfloat16),
                            pltpu.VMEM((slot_count, 2 * LB, 2 * bins), jnp.float32),
                            pltpu.VMEM((bins, CHUNK), jnp.float32), pltpu.VMEM((bins, CHUNK), jnp.float32)],
        ),
        compiler_params=pltpu.CompilerParams(dimension_semantics=("arbitrary",)),
    )(lag_blocks[0], block_count, wpad, *tables, *refparts)
    return out[None]


def solution(mesh):
    placed = (
        P("beam", None, None, "seg"),
        P("beam", None, None, "seg"),
        P(),
        P("beam"),
        P("beam", None),
        P("beam"),
    )
    return jax.shard_map(
        shards,
        mesh=mesh,
        in_specs=placed,
        out_specs=P("beam", None, None, None, "seg"),
        check_vma=False,
    )
```

```python
import functools
import math

import jax
import jax.numpy as jnp
from jax import lax
from jax.experimental import pallas as pl
from jax.experimental.pallas import tpu as pltpu
from jax.sharding import PartitionSpec as P

LB = 128
NLB = 8
DOP = 256
CHUNK = 2048
PIECE = 1024


def phase_rows(freqs, times, window_len):
    turns = jnp.mod(freqs[:, None] * times[None, :], window_len)
    angle = turns.astype(jnp.float32) * (2.0 * math.pi / window_len)
    return jnp.cos(angle), jnp.sin(angle)


def reverse_rows(x):
    n = x.shape[0]
    rows = lax.broadcasted_iota(jnp.int32, (n, n), 0)
    cols = lax.broadcasted_iota(jnp.int32, (n, n), 1)
    flip = jnp.where(rows + cols == n - 1, 1.0, 0.0).astype(jnp.bfloat16)
    high = x.astype(jnp.bfloat16)
    rest = x - high.astype(jnp.float32)
    mid = rest.astype(jnp.bfloat16)
    low = (rest - mid.astype(jnp.float32)).astype(jnp.bfloat16)
    turn = lambda piece: jnp.dot(flip, piece, preferred_element_type=jnp.float32)
    return (turn(high) + turn(mid)) + turn(low)


def caf_kernel(blocks_ref, count_ref, wpad_ref, cos_ref, sin_ref, *rest, parts, chunks, slots, span, steps,
               groups, norm):
    ref_refs = rest[:parts]
    out_ref, first_buf, second_buf, acc, bc_ref, bs_ref = rest[parts:]
    def column(ref, lane):
        tail = ref[:, LB:]
        pick = lax.broadcasted_iota(jnp.int32, tail.shape, 1) == lane
        return jnp.sum(jnp.where(pick, tail, 0.0), axis=1, keepdims=True)

    pair = pl.program_id(0)
    lanes = PIECE + LB
    pieces = [(comp, i) for comp in range(2) for i in range(span // PIECE)]
    share = -(-len(pieces) // chunks)

    def build_piece(step, comp, i, dst):
        v0 = i * PIECE
        win = wpad_ref[step, comp:comp + 1, v0:v0 + lanes]
        tile = jnp.broadcast_to(win, (LB, lanes))
        rolled = pltpu.roll(tile, lanes - LB + 1, 1, stride=1, stride_axis=0)
        dst[comp * LB:(comp + 1) * LB, v0:v0 + PIECE] = rolled[:, :PIECE].astype(jnp.bfloat16)

    @pl.when(pair == 0)
    def _():
        acc[...] = jnp.zeros_like(acc)
        l_c = cos_ref[:, :LB]
        l_s = sin_ref[:, :LB]
        for i in range(CHUNK // LB):
            h_c = jnp.broadcast_to(column(cos_ref, groups + i), (LB, LB))
            h_s = jnp.broadcast_to(column(sin_ref, groups + i), (LB, LB))
            bc_ref[:, i * LB:(i + 1) * LB] = h_c * l_c - h_s * l_s
            bs_ref[:, i * LB:(i + 1) * LB] = h_s * l_c + h_c * l_s
        for comp, i in pieces:
            build_piece(0, comp, i, first_buf)

    offsets = [jnp.maximum(blocks_ref[q], 0) * LB for q in range(slots)]

    def one_step(step, cur, nxt, next_step):
        for c in range(chunks):
            g = step * chunks + c
            rr = ref_refs[0][g].astype(jnp.float32)
            for extra in ref_refs[1:]:
                rr = rr + extra[g].astype(jnp.float32)
            r_re = rr[0:1, :]
            r_im = rr[1:2, :]
            a_c = jnp.broadcast_to(column(cos_ref, g), (LB, CHUNK))
            a_s = jnp.broadcast_to(column(sin_ref, g), (LB, CHUNK))
            b_c = bc_ref[...]
            b_s = bs_ref[...]
            cos_part = a_c * b_c - a_s * b_s
            sine_part = a_s * b_c + a_c * b_s
            c_re = (r_re * cos_part - r_im * sine_part).astype(jnp.bfloat16)
            c_im = (0.0 - (r_re * sine_part + r_im * cos_part)).astype(jnp.bfloat16)
            coef = jnp.concatenate([c_re, c_im], axis=0)
            for q in range(slots):
                off = pl.multiple_of(offsets[q] + c * CHUNK, LB)
                hank = cur[:, pl.ds(off, CHUNK)]
                acc[q] += lax.dot_general(hank, coef, (((1,), (1,)), ((), ())),
                                          preferred_element_type=jnp.float32)
            for comp, i in pieces[c * share:(c + 1) * share]:
                build_piece(next_step, comp, i, nxt)

    step = 2 * pair
    one_step(step, first_buf, second_buf, step + 1)
    one_step(step + 1, second_buf, first_buf, jnp.minimum(step + 2, steps - 1))

    @pl.when(pair == pl.num_programs(0) - 1)
    def _():
        count = count_ref[0]
        for q in range(slots):
            part = acc[q]
            re = part[:LB, :LB] - part[LB:, LB:]
            im = part[:LB, LB:] + part[LB:, :LB]
            keep = q < count
            out_ref[q, 0] = jnp.where(keep, reverse_rows(re) * norm, 0.0)
            out_ref[q, 1] = jnp.where(keep, reverse_rows(im) * norm, 0.0)


def butterfly_sum(value, axes, later=(), rider=None, stride=1):
    count = lax.axis_size(axes)
    carried = None
    while stride < count:
        radix = 4 if stride * 4 <= count else 2
        parts = []
        for m in range(1, radix):
            pairs = [(i, i ^ (m * stride)) for i in range(count)]
            if stride == 1 and m == 1 and rider is not None:
                both = lax.ppermute(jnp.concatenate([value, rider], 0), axes, pairs)
                parts.append(both[:value.shape[0]])
                carried = both[value.shape[0]:]
            else:
                parts.append(lax.ppermute(value, axes, pairs))
        if stride * radix >= count:
            return [value] + parts, later, carried
        for part in parts:
            value = value + part
        if stride == 1:
            late = (value.reshape(-1)[0] != value.reshape(-1)[0]).astype(jnp.int32)
            later = jax.tree.map(lambda x: x + late.astype(x.dtype), later)
        stride *= radix
    return [value], later, carried


def seg_join(half, axis):
    count = lax.axis_size(axis)
    parts = lax.all_gather(half, axis, axis=half.ndim - 1, tiled=True) if count != 2 else None
    if parts is not None:
        return parts
    other = lax.ppermute(half, axis, [(0, 1), (1, 0)])
    first = lax.axis_index(axis) == 0
    return jnp.where(first, jnp.concatenate([half, other], -1), jnp.concatenate([other, half], -1))


def shards(surveillance, reference_blocks, owner_index, doppler_start, lag_blocks, block_count):
    segments = lax.axis_size("seg")
    seg_place = lax.axis_index("seg")
    beam_place = lax.axis_index("beam")
    seg_len = surveillance.shape[3]
    step_count = surveillance.shape[2]
    step_len = seg_len * segments
    window_len = step_count * step_len
    slot_count = lag_blocks.shape[1]
    rim_len = NLB * LB
    bins = DOP // segments
    chunks = step_len // CHUNK

    mine = (owner_index == beam_place)[None, :, None]
    local = jnp.where(mine, reference_blocks[0], jnp.zeros_like(reference_blocks[0]))
    group = lax.axis_size(("beam", "seg"))
    if segments == 2 and group >= 16 and not group & (group - 1) and seg_len == CHUNK:
        axes = ("beam", "seg")
        first = seg_place == 0
        own = jnp.transpose(local, (1, 0, 2))
        mine_samples = jnp.transpose(surveillance[0], (1, 0, 2))
        swap = lambda x, m: lax.ppermute(x, axes, [(i, i ^ m) for i in range(group)])
        partner = swap(jnp.concatenate([own, mine_samples], 0), 1)
        same_half = own + swap(own, 2)
        other_half = partner[:step_count] + swap(own, 3)
        other = partner[step_count:]
        placed = jnp.where(first, jnp.stack([same_half, other_half], 1),
                           jnp.stack([other_half, same_half], 1)).reshape(-1, 2, seg_len)
        late = (placed.reshape(-1)[0] != placed.reshape(-1)[0]).astype(jnp.int32)
        first_bin = doppler_start[0]
        refparts, _, _ = butterfly_sum(placed, axes, stride=4)
        samples = jnp.where(first, jnp.concatenate([mine_samples, other], -1),
                            jnp.concatenate([other, mine_samples], -1))
    else:
        refs = seg_join(lax.psum(local, "beam"), "seg")
        refparts = [jnp.transpose(refs.reshape(2, step_count * chunks, CHUNK), (1, 0, 2))]
        samples = jnp.transpose(seg_join(surveillance[0], "seg"), (1, 0, 2))
        first_bin = doppler_start[0]

    span = step_len + rim_len
    wpad = samples.astype(jnp.float32)
    wpad = jnp.pad(wpad, ((0, 0), (0, 0), (0, span + LB - step_len)))

    freqs = first_bin + seg_place * bins + jnp.arange(bins, dtype=jnp.int32)
    times = jnp.concatenate([jnp.arange(LB, dtype=jnp.int32),
                             jnp.arange(step_count * chunks, dtype=jnp.int32) * CHUNK,
                             jnp.arange(CHUNK // LB, dtype=jnp.int32) * LB])
    cos_rows, sin_rows = phase_rows(freqs, times, window_len)
    tables = (cos_rows, sin_rows)
    assert step_count % 2 == 0
    kernel = functools.partial(caf_kernel, chunks=chunks, slots=slot_count, span=span, steps=step_count,
                               groups=step_count * chunks, parts=len(refparts),
                               norm=1.0 / math.sqrt(window_len))
    full = lambda shape: pl.BlockSpec(shape, lambda k, *_: (0,) * len(shape))
    out = pl.pallas_call(
        kernel,
        out_shape=jax.ShapeDtypeStruct((slot_count, 2, LB, bins), jnp.float32),
        grid_spec=pltpu.PrefetchScalarGridSpec(
            num_scalar_prefetch=2,
            grid=(step_count // 2,),
            in_specs=[full(wpad.shape)] + [full(t.shape) for t in tables] + [full(p.shape) for p in refparts],
            out_specs=full((slot_count, 2, LB, bins)),
            scratch_shapes=[pltpu.VMEM((2 * LB, span), jnp.bfloat16), pltpu.VMEM((2 * LB, span), jnp.bfloat16),
                            pltpu.VMEM((slot_count, 2 * LB, 2 * bins), jnp.float32),
                            pltpu.VMEM((bins, CHUNK), jnp.float32), pltpu.VMEM((bins, CHUNK), jnp.float32)],
        ),
        compiler_params=pltpu.CompilerParams(dimension_semantics=("arbitrary",)),
    )(lag_blocks[0], block_count, wpad, *tables, *refparts)
    return out[None]


def solution(mesh):
    placed = (
        P("beam", None, None, "seg"),
        P("beam", None, None, "seg"),
        P(),
        P("beam"),
        P("beam", None),
        P("beam"),
    )
    return jax.shard_map(
        shards,
        mesh=mesh,
        in_specs=placed,
        out_specs=P("beam", None, None, None, "seg"),
        check_vma=False,
    )
```
